32 devices in a mesh: dp: 2 (over core), expert: 16 (over z, y, x).
Axes of the slice: x: 2, y: 2, z: 4, core: 2. Of those that a mesh axis runs over, the one named last changes fastest.
Arguments:
- grad_out: bfloat16 [4096, 2048], P(('dp', 'expert')), may hold values from -0.59765625 to 0.59765625
- routes: int32 [4096, 8], P(('dp', 'expert')), may hold values from 0 to 15, all different within a row; in each aligned block of 128 rows (0 to 127, 128 to 255, ...) at most 96 rows name the same one
- router_probs: float32 [4096, 8], P(('dp', 'expert')), may hold values from 0.02 to 1
- saved_hidden: bfloat16 [16, 2, 1536, 768], P('expert', 'dp'), may hold values from -1.796875 to 1.796875
- down_weight: bfloat16 [16, 768, 2048], P('expert', 'dp'), may hold values from -0.21875 to 0.21875
- moment_one: bfloat16 [16, 768, 2048], P('expert', 'dp'), may hold values from -0.59765625 to 0.59765625
- moment_two: bfloat16 [16, 768, 2048], P('expert', 'dp'), may hold values from 0.0099487305 to 0.5
- partner: int32 [16], replicated, may hold values from 0 to 15, as said below
Outputs:
- gate_grad: float32 [4096, 8], P(('dp', 'expert'))
- new_down: bfloat16 [16, 768, 2048], P('expert', 'dp')
- new_moment_one: bfloat16 [16, 768, 2048], P('expert', 'dp')
- new_moment_two: bfloat16 [16, 768, 2048], P('expert', 'dp')
The draws below stay inside these ranges and needn't reach their ends.
Inputs may be any that keep to these rules, and one draw needn't show every extreme that they name: `routes`: each row names 8 different experts. Among the 128 rows of one device no expert is named more than 96 times, and on some device an expert is named exactly 96 times. partner[partner[i]] = i, and partner[i] is either i or differs from i in exactly one bit.
All inputs are finite; a program needn't handle non-finite values.
Results may differ from the reference program's by a relative error of at most 0.0055.
Values may be sent and summed in bfloat16 or wider, within the bound.
No kernel may reach another device: no remote copies, remote signals or barrier semaphores. Data moves between devices by JAX's collectives and lax.ppermute only.
A program may use at most 128 MiB of HBM per device.

```python
import math
import jax
import jax.numpy as jnp
import numpy as np
from jax import lax

D = 2048
FF = 768
TOPK = 8
TOK_DEV = 128
EXPERTS = 16
CAP = 96
SLOTS = 1536
TOKENS = 4096
N_DP = 2
N_EXPERT = 16


def draw_partner(key, part):
    positions = jnp.arange(EXPERTS, dtype=jnp.int32)
    matched = jnp.zeros((EXPERTS,), jnp.bool_)
    partner = positions
    for bit_level in range(EXPERTS.bit_length() - 1):
        mask_bit = 1 << bit_level
        paired = jnp.bitwise_xor(positions, mask_bit)
        coin_flip = jax.random.randint(jax.random.fold_in(key, 17 + bit_level), (EXPERTS,), 0, 3)
        lower_end = jnp.minimum(positions, paired)
        chosen = coin_flip[lower_end] == 0
        usable = chosen & jnp.logical_not(matched) & jnp.logical_not(matched[paired])
        partner = jnp.where(usable, paired, partner)
        matched = matched | usable
    return partner.astype(jnp.int32)


def steps_of(stream_key, shape, cuts, least, high):
    level, own = 1.0, jax.random.fold_in(stream_key, 6)
    for axis_at, blocks in cuts:
        draws = jnp.exp(jax.random.uniform(jax.random.fold_in(own, axis_at), (blocks,), jnp.float32, least / len(cuts), high / len(cuts)))
        level = level * jnp.repeat(draws, shape[axis_at] // blocks).reshape([-1 if axis == axis_at else 1 for axis in range(len(shape))])
    return level


def deal_out(key, own, number, rows, number_of, top, limit, slope):
    ranking = jax.random.permutation(key, number_of)
    crowded, ordinary = portions_of(number_of, rows * top, limit, slope, True), portions_of(number_of, rows * top, limit, slope, False)
    places = jnp.arange(number_of)

    def named(tallies, offset_by):
        used = int((tallies > 0).sum())
        fixed = max(1, used // 4)
        shifted = fixed + (places - fixed + offset_by * (used - fixed)) % max(1, number_of - fixed)
        return jnp.zeros((number_of,), jnp.int32).at[ranking[jnp.where(places < fixed, places, shifted)]].set(jnp.asarray(tallies, jnp.int32))

    tallies = jnp.where(number % 4 == 0, named(crowded, number // 4), named(ordinary, number - number // 4 - 1))
    mixed = jax.random.permutation(jax.random.fold_in(own, 3), number_of)
    source_of, taker = mixed[0:number_of // 2 * 2:2], mixed[1:number_of // 2 * 2:2]
    room = jnp.minimum(tallies[source_of] - 1, limit - tallies[taker]) // 2
    room = jnp.where((source_of == ranking[0]) | (taker == ranking[0]) | (tallies[taker] == 0), 0, jnp.maximum(room, 0))
    shifted = jax.random.randint(jax.random.fold_in(own, 4), (number_of // 2,), 0, 1 << 20) % (room + 1)
    tallies = tallies.at[source_of].add(-shifted).at[taker].add(shifted)
    members = jnp.searchsorted(jnp.cumsum(tallies), jnp.arange(rows * top), side="right").astype(jnp.int32)
    grid = members.reshape(top, rows).T
    grid = grid[jax.random.permutation(jax.random.fold_in(own, 1), rows)]
    offset_by = jax.random.randint(jax.random.fold_in(own, 2), (rows, 1), 0, top)
    return jnp.take_along_axis(grid, (jnp.arange(top)[None, :] + offset_by) % top, axis=1)


def portions_of(number_of, total, reach, slope, full):
    weights = [(1 << 20) // math.isqrt(standing ** slope) + 1 for standing in range(1, number_of + 1)]
    largest = reach if full else min(reach, max(-(-total // number_of), total * weights[0] // sum(weights)))
    least = 1 if total - largest >= number_of - 1 else 0
    counts, rest = [largest] + [least] * (number_of - 1), total - largest - least * (number_of - 1)
    while rest > 0:
        movable = [i for i in range(1, number_of) if counts[i] < largest] or [i for i in range(1, number_of) if counts[i] < reach]
        whole, budget = sum([weights[i] for i in movable]), rest
        for i in movable:
            addition = min(reach - counts[i], max(1, budget * weights[i] // whole), rest)
            counts[i] = counts[i] + addition
            rest = rest - addition
    return np.array(counts)


def gaussian(own_key, shape, width, most, pieces=(), held_as=jnp.bfloat16):
    values = jax.random.normal(own_key, shape, jnp.float32) * width
    if len(pieces) > 0:
        values = steps_of(own_key, shape, pieces, -0.22, 0.18) * values
    return jnp.clip(values, min=-most, max=most).astype(held_as)


def setup_inputs(seed: int = 0) -> dict:
    key_of = jax.random.split(jax.random.key(seed), 9)
    grad_out = gaussian(key_of[0], (TOKENS, D), 0.1, 0.59765625, ((0, 32),))
    routes_keys = jax.random.split(jax.random.fold_in(key_of[1], 1), TOKENS // TOK_DEV)
    routes_turns = jax.random.permutation(jax.random.fold_in(key_of[1], 3), TOKENS // TOK_DEV)
    routes = jax.vmap(lambda own, number: deal_out(jax.random.fold_in(key_of[1], 2), own, number, TOK_DEV, EXPERTS, TOPK, CAP, 2))(routes_keys, routes_turns).reshape((TOKENS, TOPK))
    router_probs = jnp.clip(0.02 + 0.98 * jax.random.uniform(key_of[2], (TOKENS, TOPK), jnp.float32) ** steps_of(key_of[2], (TOKENS, TOPK), ((0, 32),), -0.2, 0.2), 0.02, 1.0)
    saved_hidden = gaussian(key_of[3], (EXPERTS, N_DP, SLOTS, FF), 0.3, 1.796875, ((0, 16), (1, 2)))
    down_weight = gaussian(key_of[4], (EXPERTS, FF, D), FF ** -0.5, 0.21875, ((0, 16), (1, 2)))
    moment_one = gaussian(key_of[5], (EXPERTS, FF, D), 0.1, 0.59765625, ((0, 16), (1, 2)))
    moment_two = jnp.clip(jnp.exp(math.log(0.5) - 3.9171631 * jax.random.uniform(key_of[6], (EXPERTS, FF, D), jnp.float32) ** steps_of(key_of[6], (EXPERTS, FF, D), ((0, 16), (1, 2)), -0.2, 0.2)), 0.0099487305, 0.5).astype(jnp.bfloat16)
    partner = draw_partner(jax.random.fold_in(key_of[8], 71), 0)
    return dict(grad_out=grad_out, routes=routes, router_probs=router_probs, saved_hidden=saved_hidden, down_weight=down_weight, moment_one=moment_one, moment_two=moment_two, partner=partner)


beta_one = 0.9
beta_two = 0.95
learn_rate = 0.001
weight_decay = 0.1
adam_epsilon = 1e-08
step_count = 1000

def block_rank(block_routes):
    expert_iota = jnp.arange(EXPERTS, dtype=jnp.int32)
    onehot = (block_routes[:, None] == expert_iota[None, :]).astype(jnp.int32)
    running = jnp.cumsum(onehot, axis=0)
    return lax.optimization_barrier(jnp.sum(running * onehot, axis=1)) - 1

def adam_update(weight, moment_first, moment_second, grad_sum):
    first_new = beta_one * moment_first.astype(jnp.float32) + (1.0 - beta_one) * grad_sum
    second_new = beta_two * moment_second.astype(jnp.float32) + (1.0 - beta_two) * grad_sum * grad_sum
    corr_one = 1.0 - beta_one ** step_count
    corr_two = 1.0 - beta_two ** step_count
    weight_full = weight.astype(jnp.float32)
    direction = first_new / corr_one / (jnp.sqrt(second_new / corr_two) + adam_epsilon)
    updated = weight_full - learn_rate * (direction + weight_decay * weight_full)
    return (updated.astype(jnp.bfloat16), first_new.astype(jnp.bfloat16), second_new.astype(jnp.bfloat16))

def reference(grad_out, routes, router_probs, saved_hidden, down_weight, moment_one, moment_two, partner):
    block_count = N_DP * N_EXPERT
    pair_count = TOKENS * TOPK
    slot_rank = lax.map(block_rank, routes.reshape(block_count, TOK_DEV * TOPK)).reshape(pair_count)
    expert_flat = routes.reshape(pair_count)
    token_index = jnp.arange(pair_count, dtype=jnp.int32) // TOPK
    block_index = token_index // TOK_DEV
    data_group = block_index // N_EXPERT
    source = block_index % N_EXPERT
    slot_index = source * CAP + slot_rank
    global_slot = ((expert_flat * N_DP + data_group) * SLOTS + slot_index).astype(jnp.int32)
    slot_total = EXPERTS * N_DP * SLOTS
    prob_sum = lax.optimization_barrier(jnp.sum(router_probs, axis=1, keepdims=True))
    gate_share = router_probs / prob_sum
    gate_low = gate_share.astype(jnp.bfloat16)
    token_of = jnp.zeros((slot_total,), jnp.int32).at[global_slot].set(token_index).reshape(EXPERTS, N_DP, SLOTS)
    filled = jnp.zeros((slot_total,), jnp.int32).at[global_slot].set(1).reshape(EXPERTS, N_DP, SLOTS)
    gate_of = jnp.zeros((slot_total,), jnp.bfloat16).at[global_slot].set(gate_low.reshape(pair_count)).reshape(EXPERTS, N_DP, SLOTS)

    def per_expert(operands):
        token_rows, slot_used, slot_gate, hidden, weight, moment_first, moment_second = operands
        grad_sum = jnp.zeros((FF, D), jnp.float32)
        products = []
        for group_index in range(N_DP):
            picked = grad_out[token_rows[group_index]]
            dispatched = jnp.where(slot_used[group_index][:, None] > 0, picked, jnp.zeros_like(picked))
            scaled = slot_gate[group_index][:, None] * dispatched
            projected = lax.dot_general(dispatched, weight, (((1,), (1,)), ((), ())), preferred_element_type=jnp.float32)
            products.append(lax.optimization_barrier(jnp.sum(hidden[group_index].astype(jnp.float32) * projected, axis=1)))
            grad_sum = grad_sum + lax.dot_general(hidden[group_index], scaled, (((0,), (0,)), ((), ())), preferred_element_type=jnp.float32)
        updated, first_new, second_new = adam_update(weight, moment_first, moment_second, grad_sum)
        return (updated, first_new, second_new, jnp.stack(products))
    updated, first_new, second_new, products = lax.map(per_expert, (token_of, filled, gate_of, saved_hidden, down_weight, moment_one, moment_two))
    new_down = jnp.take(updated, partner, axis=0)
    new_one = jnp.take(first_new, partner, axis=0)
    new_two = jnp.take(second_new, partner, axis=0)
    answer = products.reshape(slot_total)[global_slot].reshape(TOKENS, TOPK)
    gate_grad = (answer - lax.optimization_barrier(jnp.sum(gate_share * answer, axis=1, keepdims=True))) / prob_sum
    return (gate_grad, new_down, new_one, new_two)
```

```python
import jax
import jax.numpy as jnp
from jax import lax
from jax.sharding import PartitionSpec as P

beta_one = 0.9
beta_two = 0.95
learn_rate = 0.001
weight_decay = 0.1
adam_epsilon = 1e-08
step_count = 1000

gather_limit_bytes = 16 * 1024 * 1024


def adam_update(weight, moment_first, moment_second, grad_sum):
    first_new = beta_one * moment_first.astype(jnp.float32) + (1.0 - beta_one) * grad_sum
    second_new = (
        beta_two * moment_second.astype(jnp.float32) + (1.0 - beta_two) * grad_sum * grad_sum
    )
    corr_one = 1.0 - beta_one**step_count
    corr_two = 1.0 - beta_two**step_count
    weight_full = weight.astype(jnp.float32)
    direction = first_new / corr_one / (jnp.sqrt(second_new / corr_two) + adam_epsilon)
    updated = weight_full - learn_rate * (direction + weight_decay * weight_full)
    return (
        updated.astype(jnp.bfloat16),
        first_new.astype(jnp.bfloat16),
        second_new.astype(jnp.bfloat16),
    )


def block_ranks(hit):
    return jnp.cumsum(hit.astype(jnp.int32), axis=-1) - 1


def slot_onehot(hit, rank, capacity):
    slot_iota = jnp.arange(capacity, dtype=jnp.int32)
    return hit[..., None, :] & (rank[..., None, :] == slot_iota[:, None])


def on_device(
    grad_out, routes, router_probs, saved_hidden, down_weight, moment_one, moment_two, partner
):
    tok_rows, top_count = routes.shape
    width = grad_out.shape[1]
    axis_size = lax.axis_size("expert")
    me = lax.axis_index("expert")
    expert_count = partner.shape[0]
    capacity = 3 * tok_rows * top_count // (2 * expert_count)
    slot_count = capacity * axis_size

    weight = down_weight[0]
    weight_full = lax.all_gather(weight, "dp", axis=0, tiled=True)
    hidden = saved_hidden[0, 0]

    prob_sum = jnp.sum(router_probs, axis=1, keepdims=True)
    gate_share = router_probs / prob_sum
    gate_low = gate_share.astype(jnp.bfloat16)

    expert_iota = jnp.arange(expert_count, dtype=jnp.int32)
    local_hit = jnp.any(routes[:, :, None] == expert_iota[None, None, :], axis=1)
    local_rank = block_ranks(local_hit.T).T
    pair_rank = jnp.take_along_axis(local_rank, routes, axis=1)

    gather_bytes = axis_size * tok_rows * width * grad_out.dtype.itemsize
    if gather_bytes <= gather_limit_bytes:
        packed = jnp.concatenate([routes.astype(jnp.float32), router_probs], axis=1)
        packed_all = lax.all_gather(packed, "expert", axis=0, tiled=True)
        grad_all = lax.all_gather(grad_out, "expert", axis=0, tiled=True)
        routes_all = packed_all[:, :top_count].astype(jnp.int32)
        probs_all = packed_all[:, top_count:]
        gate_all = (probs_all / jnp.sum(probs_all, axis=1, keepdims=True)).astype(jnp.bfloat16)
        hit_k = routes_all == me
        hit = jnp.any(hit_k, axis=1).reshape(axis_size, tok_rows)
        gate_tok = jnp.sum(
            jnp.where(hit_k, gate_all.astype(jnp.float32), 0.0), axis=1
        ).reshape(axis_size, tok_rows)
        onehot = slot_onehot(hit, block_ranks(hit), capacity)
        dispatched = jnp.einsum(
            "sjt,std->sjd",
            onehot.astype(jnp.bfloat16),
            grad_all.reshape(axis_size, tok_rows, width),
            preferred_element_type=jnp.float32,
        ).astype(jnp.bfloat16)
        slot_gate = jnp.sum(
            jnp.where(onehot, gate_tok[:, None, :], 0.0), axis=2
        ).astype(jnp.bfloat16)
    else:
        gate_pair = jnp.sum(
            jnp.where(
                routes[:, :, None] == expert_iota[None, None, :],
                gate_low.astype(jnp.float32)[:, :, None],
                0.0,
            ),
            axis=1,
        )
        onehot = slot_onehot(local_hit.T, local_rank.T, capacity)
        send_rows = jnp.einsum(
            "ejt,td->ejd",
            onehot.astype(jnp.bfloat16),
            grad_out,
            preferred_element_type=jnp.float32,
        ).astype(jnp.bfloat16)
        send_gate = jnp.sum(jnp.where(onehot, gate_pair.T[:, None, :], 0.0), axis=2).astype(
            jnp.bfloat16
        )
        dispatched = lax.all_to_all(send_rows, "expert", split_axis=0, concat_axis=0, tiled=True)
        slot_gate = lax.all_to_all(send_gate, "expert", split_axis=0, concat_axis=0, tiled=True)

    dispatched = dispatched.reshape(slot_count, width)
    slot_gate = slot_gate.reshape(slot_count)
    scaled = slot_gate[:, None] * dispatched
    projected = lax.dot_general(
        dispatched,
        weight_full,
        (((1,), (1,)), ((), ())),
        preferred_element_type=jnp.float32,
    )
    products = jnp.sum(hidden.astype(jnp.float32) * projected, axis=1)
    grad_sum = lax.psum_scatter(
        lax.dot_general(
            hidden, scaled, (((0,), (0,)), ((), ())), preferred_element_type=jnp.float32
        ).astype(jnp.bfloat16),
        "dp",
        scatter_dimension=0,
        tiled=True,
    ).astype(jnp.float32)
    returned = lax.all_to_all(
        products.reshape(axis_size, capacity), "expert", split_axis=0, concat_axis=0, tiled=True
    )
    answer = returned.reshape(-1)[routes * capacity + pair_rank]
    gate_grad = (answer - jnp.sum(gate_share * answer, axis=1, keepdims=True)) / prob_sum

    outputs = adam_update(weight, moment_one[0], moment_two[0], grad_sum)

    mine = partner[me]
    levels = axis_size.bit_length() - 1
    which = jnp.int32(0)
    cases = [outputs]
    for level in range(levels):
        flip = 1 << level
        which = which + jnp.where(mine == (me ^ flip), level + 1, 0).astype(jnp.int32)
        cases.append(
            lax.ppermute(outputs, "expert", perm=[(i, i ^ flip) for i in range(axis_size)])
        )
    landed = [
        lax.select_n(which, *[case[index] for case in cases]) for index in range(3)
    ]
    return (gate_grad, landed[0][None], landed[1][None], landed[2][None])


def solution(mesh):
    in_specs = (
        P(("dp", "expert"), None),
        P(("dp", "expert"), None),
        P(("dp", "expert"), None),
        P("expert", "dp", None, None),
        P("expert", "dp", None),
        P("expert", "dp", None),
        P("expert", "dp", None),
        P(),
    )
    out_specs = (
        P(("dp", "expert"), None),
        P("expert", "dp", None),
        P("expert", "dp", None),
        P("expert", "dp", None),
    )
    return jax.shard_map(
        on_device, mesh=mesh, in_specs=in_specs, out_specs=out_specs, check_vma=False
    )
```

```python
import jax
import jax.numpy as jnp
from jax import lax
from jax.sharding import PartitionSpec as P

beta_one = 0.9
beta_two = 0.95
learn_rate = 0.001
weight_decay = 0.1
adam_epsilon = 1e-08
step_count = 1000

gather_limit_bytes = 16 * 1024 * 1024


def adam_update(weight, moment_first, moment_second, grad_sum):
    first_new = beta_one * moment_first.astype(jnp.float32) + (1.0 - beta_one) * grad_sum
    second_new = (
        beta_two * moment_second.astype(jnp.float32) + (1.0 - beta_two) * grad_sum * grad_sum
    )
    corr_one = 1.0 - beta_one**step_count
    corr_two = 1.0 - beta_two**step_count
    weight_full = weight.astype(jnp.float32)
    direction = first_new / corr_one / (jnp.sqrt(second_new / corr_two) + adam_epsilon)
    updated = weight_full - learn_rate * (direction + weight_decay * weight_full)
    return (
        updated.astype(jnp.bfloat16),
        first_new.astype(jnp.bfloat16),
        second_new.astype(jnp.bfloat16),
    )


def block_ranks(hit):
    return jnp.cumsum(hit.astype(jnp.int32), axis=-1) - 1


def slot_onehot(hit, rank, capacity):
    slot_iota = jnp.arange(capacity, dtype=jnp.int32)
    return hit[..., None, :] & (rank[..., None, :] == slot_iota[:, None])


def on_device(
    grad_out, routes, router_probs, saved_hidden, down_weight, moment_one, moment_two, partner
):
    tok_rows, top_count = routes.shape
    width = grad_out.shape[1]
    axis_size = lax.axis_size("expert")
    me = lax.axis_index("expert")
    expert_count = partner.shape[0]
    capacity = 3 * tok_rows * top_count // (2 * expert_count)
    slot_count = capacity * axis_size

    weight = down_weight[0]
    weight_full = lax.all_gather(weight, "dp", axis=0, tiled=True)

    mine = partner[me]
    levels = axis_size.bit_length() - 1
    which = jnp.int32(0)
    for level in range(levels):
        which = which + jnp.where(mine == (me ^ (1 << level)), level + 1, 0).astype(jnp.int32)

    def relocate(arrays):
        cases = [arrays]
        for level in range(levels):
            flip = 1 << level
            cases.append(
                lax.ppermute(arrays, "expert", perm=[(i, i ^ flip) for i in range(axis_size)])
            )
        return [lax.select_n(which, *[case[k] for case in cases]) for k in range(len(arrays))]

    moved = relocate((weight, moment_one[0], moment_two[0]))
    hidden = saved_hidden[0, 0]

    prob_sum = jnp.sum(router_probs, axis=1, keepdims=True)
    gate_share = router_probs / prob_sum
    gate_low = gate_share.astype(jnp.bfloat16)

    expert_iota = jnp.arange(expert_count, dtype=jnp.int32)
    local_hit = jnp.any(routes[:, :, None] == expert_iota[None, None, :], axis=1)
    local_rank = block_ranks(local_hit.T).T
    pair_rank = jnp.take_along_axis(local_rank, routes, axis=1)

    gather_bytes = axis_size * tok_rows * width * grad_out.dtype.itemsize
    if gather_bytes <= gather_limit_bytes:
        packed = jnp.concatenate([routes.astype(jnp.bfloat16), gate_low], axis=1)
        extended = jnp.concatenate(
            [grad_out, packed.reshape(-1, width).astype(grad_out.dtype)], axis=0
        )
        extended_all = lax.all_gather(extended, "expert", axis=0, tiled=False)
        grad_all = extended_all[:, :tok_rows]
        packed_all = extended_all[:, tok_rows:].reshape(axis_size * tok_rows, 2 * top_count)
        grad_all, moved = lax.optimization_barrier((grad_all, moved))
        routes_all = packed_all[:, :top_count].astype(jnp.int32)
        gate_all = packed_all[:, top_count:]
        hit_k = routes_all == me
        hit = jnp.any(hit_k, axis=1).reshape(axis_size, tok_rows)
        gate_tok = jnp.sum(
            jnp.where(hit_k, gate_all.astype(jnp.float32), 0.0), axis=1
        ).reshape(axis_size, tok_rows)
        onehot = slot_onehot(hit, block_ranks(hit), capacity)
        dispatched = jnp.einsum(
            "sjt,std->sjd",
            onehot.astype(jnp.bfloat16),
            grad_all,
            preferred_element_type=jnp.float32,
        ).astype(jnp.bfloat16)
        slot_gate = jnp.sum(
            jnp.where(onehot, gate_tok[:, None, :], 0.0), axis=2
        ).astype(jnp.bfloat16)
    else:
        gate_pair = jnp.sum(
            jnp.where(
                routes[:, :, None] == expert_iota[None, None, :],
                gate_low.astype(jnp.float32)[:, :, None],
                0.0,
            ),
            axis=1,
        )
        onehot = slot_onehot(local_hit.T, local_rank.T, capacity)
        send_rows = jnp.einsum(
            "ejt,td->ejd",
            onehot.astype(jnp.bfloat16),
            grad_out,
            preferred_element_type=jnp.float32,
        ).astype(jnp.bfloat16)
        send_gate = jnp.sum(jnp.where(onehot, gate_pair.T[:, None, :], 0.0), axis=2).astype(
            jnp.bfloat16
        )
        dispatched = lax.all_to_all(send_rows, "expert", split_axis=0, concat_axis=0, tiled=True)
        slot_gate = lax.all_to_all(send_gate, "expert", split_axis=0, concat_axis=0, tiled=True)

    dispatched = dispatched.reshape(slot_count, width)
    slot_gate = slot_gate.reshape(slot_count)
    scaled = slot_gate[:, None] * dispatched
    projected = lax.dot_general(
        dispatched,
        weight_full,
        (((1,), (1,)), ((), ())),
        preferred_element_type=jnp.float32,
    )
    products = jnp.sum(hidden.astype(jnp.float32) * projected, axis=1)
    grad_sum = lax.psum_scatter(
        lax.dot_general(
            hidden, scaled, (((0,), (0,)), ((), ())), preferred_element_type=jnp.float32
        ).astype(jnp.bfloat16),
        "dp",
        scatter_dimension=0,
        tiled=True,
    )
    moved_grad = relocate((grad_sum,))
    returned = lax.all_gather(products, "expert", axis=0, tiled=False)
    answer = returned.reshape(-1)[routes * slot_count + me * capacity + pair_rank]
    gate_grad = (answer - jnp.sum(gate_share * answer, axis=1, keepdims=True)) / prob_sum

    outputs = adam_update(moved[0], moved[1], moved[2], moved_grad[0].astype(jnp.float32))
    return (gate_grad, outputs[0][None], outputs[1][None], outputs[2][None])


def solution(mesh):
    in_specs = (
        P(("dp", "expert"), None),
        P(("dp", "expert"), None),
        P(("dp", "expert"), None),
        P("expert", "dp", None, None),
        P("expert", "dp", None),
        P("expert", "dp", None),
        P("expert", "dp", None),
        P(),
    )
    out_specs = (
        P(("dp", "expert"), None),
        P("expert", "dp", None),
        P("expert", "dp", None),
        P("expert", "dp", None),
    )
    return jax.shard_map(
        on_device, mesh=mesh, in_specs=in_specs, out_specs=out_specs, check_vma=False
    )
```

```python
import jax
import jax.numpy as jnp
from jax import lax
from jax.sharding import PartitionSpec as P

beta_one = 0.9
beta_two = 0.95
learn_rate = 0.001
weight_decay = 0.1
adam_epsilon = 1e-08
step_count = 1000

gather_limit_bytes = 16 * 1024 * 1024


def adam_update(weight, moment_first, moment_second, grad_sum):
    first_new = beta_one * moment_first.astype(jnp.float32) + (1.0 - beta_one) * grad_sum
    second_new = (
        beta_two * moment_second.astype(jnp.float32) + (1.0 - beta_two) * grad_sum * grad_sum
    )
    corr_one = 1.0 - beta_one**step_count
    corr_two = 1.0 - beta_two**step_count
    weight_full = weight.astype(jnp.float32)
    direction = first_new / corr_one / (jnp.sqrt(second_new / corr_two) + adam_epsilon)
    updated = weight_full - learn_rate * (direction + weight_decay * weight_full)
    return (
        updated.astype(jnp.bfloat16),
        first_new.astype(jnp.bfloat16),
        second_new.astype(jnp.bfloat16),
    )


def block_ranks(hit):
    return jnp.cumsum(hit.astype(jnp.int32), axis=-1) - 1


def slot_onehot(hit, rank, capacity):
    slot_iota = jnp.arange(capacity, dtype=jnp.int32)
    return hit[..., None, :] & (rank[..., None, :] == slot_iota[:, None])


def on_device(
    grad_out, routes, router_probs, saved_hidden, down_weight, moment_one, moment_two, partner
):
    tok_rows, top_count = routes.shape
    width = grad_out.shape[1]
    axis_size = lax.axis_size("expert")
    me = lax.axis_index("expert")
    expert_count = partner.shape[0]
    capacity = 3 * tok_rows * top_count // (2 * expert_count)
    slot_count = capacity * axis_size

    weight = down_weight[0]
    weight_full = lax.all_gather(weight, "dp", axis=0, tiled=True)

    hidden = saved_hidden[0, 0]

    prob_sum = jnp.sum(router_probs, axis=1, keepdims=True)
    gate_share = router_probs / prob_sum
    gate_low = gate_share.astype(jnp.bfloat16)

    expert_iota = jnp.arange(expert_count, dtype=jnp.int32)
    local_hit = jnp.any(routes[:, :, None] == expert_iota[None, None, :], axis=1)
    local_rank = block_ranks(local_hit.T).T
    pair_rank = jnp.take_along_axis(local_rank, routes, axis=1)

    gather_bytes = axis_size * tok_rows * width * grad_out.dtype.itemsize
    if gather_bytes <= gather_limit_bytes:
        packed = jnp.concatenate([routes.astype(jnp.bfloat16), gate_low], axis=1)
        extended = jnp.concatenate(
            [grad_out, packed.reshape(-1, width).astype(grad_out.dtype)], axis=0
        )
        extended_all = lax.all_gather(extended, "expert", axis=0, tiled=False)
        grad_all = extended_all[:, :tok_rows]
        packed_all = extended_all[:, tok_rows:].reshape(axis_size * tok_rows, 2 * top_count)
        routes_all = packed_all[:, :top_count].astype(jnp.int32)
        gate_all = packed_all[:, top_count:]
        hit_k = routes_all == me
        hit = jnp.any(hit_k, axis=1).reshape(axis_size, tok_rows)
        gate_tok = jnp.sum(
            jnp.where(hit_k, gate_all.astype(jnp.float32), 0.0), axis=1
        ).reshape(axis_size, tok_rows)
        onehot = slot_onehot(hit, block_ranks(hit), capacity)
        dispatched = jnp.einsum(
            "sjt,std->sjd",
            onehot.astype(jnp.bfloat16),
            grad_all,
            preferred_element_type=jnp.float32,
        ).astype(jnp.bfloat16)
        slot_gate = jnp.sum(
            jnp.where(onehot, gate_tok[:, None, :], 0.0), axis=2
        ).astype(jnp.bfloat16)
    else:
        gate_pair = jnp.sum(
            jnp.where(
                routes[:, :, None] == expert_iota[None, None, :],
                gate_low.astype(jnp.float32)[:, :, None],
                0.0,
            ),
            axis=1,
        )
        onehot = slot_onehot(local_hit.T, local_rank.T, capacity)
        send_rows = jnp.einsum(
            "ejt,td->ejd",
            onehot.astype(jnp.bfloat16),
            grad_out,
            preferred_element_type=jnp.float32,
        ).astype(jnp.bfloat16)
        send_gate = jnp.sum(jnp.where(onehot, gate_pair.T[:, None, :], 0.0), axis=2).astype(
            jnp.bfloat16
        )
        dispatched = lax.all_to_all(send_rows, "expert", split_axis=0, concat_axis=0, tiled=True)
        slot_gate = lax.all_to_all(send_gate, "expert", split_axis=0, concat_axis=0, tiled=True)

    dispatched = dispatched.reshape(slot_count, width)
    slot_gate = slot_gate.reshape(slot_count)
    scaled = slot_gate[:, None] * dispatched
    projected = lax.dot_general(
        dispatched,
        weight_full,
        (((1,), (1,)), ((), ())),
        preferred_element_type=jnp.float32,
    )
    products = jnp.sum(hidden.astype(jnp.float32) * projected, axis=1)
    grad_sum = lax.psum_scatter(
        lax.dot_general(
            hidden, scaled, (((0,), (0,)), ((), ())), preferred_element_type=jnp.float32
        ).astype(jnp.bfloat16),
        "dp",
        scatter_dimension=0,
        tiled=True,
    )
    returned = lax.all_gather(products, "expert", axis=0, tiled=False)
    answer = returned.reshape(-1)[routes * slot_count + me * capacity + pair_rank]
    gate_grad = (answer - jnp.sum(gate_share * answer, axis=1, keepdims=True)) / prob_sum

    outputs = adam_update(weight, moment_one[0], moment_two[0], grad_sum.astype(jnp.float32))
    outputs, gate_grad = lax.optimization_barrier((outputs, gate_grad))

    mine = partner[me]
    levels = axis_size.bit_length() - 1
    device_iota = jnp.arange(expert_count, dtype=jnp.int32)
    which = jnp.int32(0)
    level_mask = jnp.int32(0)
    for level in range(levels):
        which = which + jnp.where(mine == (me ^ (1 << level)), level + 1, 0).astype(jnp.int32)
        used = jnp.any(partner == (device_iota ^ (1 << level)))
        level_mask = level_mask + jnp.where(used, 1 << level, 0).astype(jnp.int32)

    def exchange(chosen):
        def run(arrays):
            cases = [arrays]
            index = jnp.int32(0)
            for position, level in enumerate(chosen):
                flip = 1 << level
                cases.append(
                    lax.ppermute(arrays, "expert", perm=[(i, i ^ flip) for i in range(axis_size)])
                )
                index = index + jnp.where(which == level + 1, position + 1, 0).astype(jnp.int32)
            if len(cases) == 1:
                return arrays
            return tuple(
                lax.select_n(index, *[case[k] for case in cases]) for k in range(len(arrays))
            )

        return run

    if levels <= 4:
        branches = [
            exchange([level for level in range(levels) if mask >> level & 1])
            for mask in range(1 << levels)
        ]
        landed = lax.switch(level_mask, branches, outputs)
    else:
        landed = exchange(list(range(levels)))(outputs)
    return (gate_grad, landed[0][None], landed[1][None], landed[2][None])


def solution(mesh):
    in_specs = (
        P(("dp", "expert"), None),
        P(("dp", "expert"), None),
        P(("dp", "expert"), None),
        P("expert", "dp", None, None),
        P("expert", "dp", None),
        P("expert", "dp", None),
        P("expert", "dp", None),
        P(),
    )
    out_specs = (
        P(("dp", "expert"), None),
        P("expert", "dp", None),
        P("expert", "dp", None),
        P("expert", "dp", None),
    )
    return jax.shard_map(
        on_device, mesh=mesh, in_specs=in_specs, out_specs=out_specs, check_vma=False
    )
```

```python
import jax
import jax.numpy as jnp
from jax import lax
from jax.sharding import PartitionSpec as P

beta_one = 0.9
beta_two = 0.95
learn_rate = 0.001
weight_decay = 0.1
adam_epsilon = 1e-08
step_count = 1000

gather_limit_bytes = 16 * 1024 * 1024


def adam_update(weight, moment_first, moment_second, grad_sum):
    first_new = beta_one * moment_first.astype(jnp.float32) + (1.0 - beta_one) * grad_sum
    second_new = (
        beta_two * moment_second.astype(jnp.float32) + (1.0 - beta_two) * grad_sum * grad_sum
    )
    corr_one = 1.0 - beta_one**step_count
    corr_two = 1.0 - beta_two**step_count
    weight_full = weight.astype(jnp.float32)
    direction = first_new / corr_one / (jnp.sqrt(second_new / corr_two) + adam_epsilon)
    updated = weight_full - learn_rate * (direction + weight_decay * weight_full)
    return (
        updated.astype(jnp.bfloat16),
        first_new.astype(jnp.bfloat16),
        second_new.astype(jnp.bfloat16),
    )


def block_ranks(hit):
    return jnp.cumsum(hit.astype(jnp.int32), axis=-1) - 1


def slot_onehot(hit, rank, capacity):
    slot_iota = jnp.arange(capacity, dtype=jnp.int32)
    return hit[..., None, :] & (rank[..., None, :] == slot_iota[:, None])


def on_device(
    grad_out, routes, router_probs, saved_hidden, down_weight, moment_one, moment_two, partner
):
    tok_rows, top_count = routes.shape
    width = grad_out.shape[1]
    axis_size = lax.axis_size("expert")
    me = lax.axis_index("expert")
    expert_count = partner.shape[0]
    capacity = 3 * tok_rows * top_count // (2 * expert_count)
    slot_count = capacity * axis_size

    weight = down_weight[0]
    weight_full = lax.all_gather(weight, "dp", axis=0, tiled=True)
    hidden = saved_hidden[0, 0]

    prob_sum = jnp.sum(router_probs, axis=1, keepdims=True)
    gate_share = router_probs / prob_sum
    gate_low = gate_share.astype(jnp.bfloat16)

    expert_iota = jnp.arange(expert_count, dtype=jnp.int32)
    local_hit = jnp.any(routes[:, :, None] == expert_iota[None, None, :], axis=1)
    local_rank = block_ranks(local_hit.T).T
    pair_rank = jnp.take_along_axis(local_rank, routes, axis=1)

    gather_bytes = axis_size * tok_rows * width * grad_out.dtype.itemsize
    if gather_bytes <= gather_limit_bytes:
        packed = jnp.concatenate([routes.astype(jnp.float32), router_probs], axis=1)
        packed_all = lax.all_gather(packed, "expert", axis=0, tiled=True)
        grad_all = lax.all_gather(grad_out, "expert", axis=0, tiled=True)
        routes_all = packed_all[:, :top_count].astype(jnp.int32)
        probs_all = packed_all[:, top_count:]
        gate_all = (probs_all / jnp.sum(probs_all, axis=1, keepdims=True)).astype(jnp.bfloat16)
        hit_k = routes_all == me
        hit = jnp.any(hit_k, axis=1).reshape(axis_size, tok_rows)
        gate_tok = jnp.sum(
            jnp.where(hit_k, gate_all.astype(jnp.float32), 0.0), axis=1
        ).reshape(axis_size, tok_rows)
        onehot = slot_onehot(hit, block_ranks(hit), capacity)
        dispatched = jnp.einsum(
            "sjt,std->sjd",
            onehot.astype(jnp.bfloat16),
            grad_all.reshape(axis_size, tok_rows, width),
            preferred_element_type=jnp.float32,
        ).astype(jnp.bfloat16)
        slot_gate = jnp.sum(
            jnp.where(onehot, gate_tok[:, None, :], 0.0), axis=2
        ).astype(jnp.bfloat16)
    else:
        gate_pair = jnp.sum(
            jnp.where(
                routes[:, :, None] == expert_iota[None, None, :],
                gate_low.astype(jnp.float32)[:, :, None],
                0.0,
            ),
            axis=1,
        )
        onehot = slot_onehot(local_hit.T, local_rank.T, capacity)
        send_rows = jnp.einsum(
            "ejt,td->ejd",
            onehot.astype(jnp.bfloat16),
            grad_out,
            preferred_element_type=jnp.float32,
        ).astype(jnp.bfloat16)
        send_gate = jnp.sum(jnp.where(onehot, gate_pair.T[:, None, :], 0.0), axis=2).astype(
            jnp.bfloat16
        )
        dispatched = lax.all_to_all(send_rows, "expert", split_axis=0, concat_axis=0, tiled=True)
        slot_gate = lax.all_to_all(send_gate, "expert", split_axis=0, concat_axis=0, tiled=True)

    dispatched = dispatched.reshape(slot_count, width)
    slot_gate = slot_gate.reshape(slot_count)
    scaled = slot_gate[:, None] * dispatched
    projected = lax.dot_general(
        dispatched,
        weight_full,
        (((1,), (1,)), ((), ())),
        preferred_element_type=jnp.float32,
    )
    products = jnp.sum(hidden.astype(jnp.float32) * projected, axis=1)
    grad_sum = lax.psum_scatter(
        lax.dot_general(
            hidden, scaled, (((0,), (0,)), ((), ())), preferred_element_type=jnp.float32
        ).astype(jnp.bfloat16),
        "dp",
        scatter_dimension=0,
        tiled=True,
    ).astype(jnp.float32)
    returned = lax.all_to_all(
        products.reshape(axis_size, capacity), "expert", split_axis=0, concat_axis=0, tiled=True
    )
    answer = returned.reshape(-1)[routes * capacity + pair_rank]
    gate_grad = (answer - jnp.sum(gate_share * answer, axis=1, keepdims=True)) / prob_sum

    outputs = adam_update(weight, moment_one[0], moment_two[0], grad_sum)
    outputs, gate_grad = lax.optimization_barrier((outputs, gate_grad))

    rows = weight.shape[0]
    lane = width // axis_size
    stacked = jnp.stack(outputs).reshape(3, rows, axis_size, lane).transpose(2, 0, 1, 3)
    outward = lax.all_to_all(stacked, "expert", split_axis=0, concat_axis=0, tiled=True)
    turned = jnp.take(outward, partner, axis=0)
    landed = lax.all_to_all(turned, "expert", split_axis=0, concat_axis=0, tiled=True)
    landed = landed.transpose(1, 2, 0, 3).reshape(3, rows, width)
    return (gate_grad, landed[0][None], landed[1][None], landed[2][None])


def solution(mesh):
    in_specs = (
        P(("dp", "expert"), None),
        P(("dp", "expert"), None),
        P(("dp", "expert"), None),
        P("expert", "dp", None, None),
        P("expert", "dp", None),
        P("expert", "dp", None),
        P("expert", "dp", None),
        P(),
    )
    out_specs = (
        P(("dp", "expert"), None),
        P("expert", "dp", None),
        P("expert", "dp", None),
        P("expert", "dp", None),
    )
    return jax.shard_map(
        on_device, mesh=mesh, in_specs=in_specs, out_specs=out_specs, check_vma=False
    )
```

```python
import jax
import jax.numpy as jnp
from jax import lax
from jax.sharding import PartitionSpec as P

beta_one = 0.9
beta_two = 0.95
learn_rate = 0.001
weight_decay = 0.1
adam_epsilon = 1e-08
step_count = 1000

gather_limit_bytes = 16 * 1024 * 1024


def adam_update(weight, moment_first, moment_second, grad_sum):
    first_new = beta_one * moment_first.astype(jnp.float32) + (1.0 - beta_one) * grad_sum
    second_new = (
        beta_two * moment_second.astype(jnp.float32) + (1.0 - beta_two) * grad_sum * grad_sum
    )
    corr_one = 1.0 - beta_one**step_count
    corr_two = 1.0 - beta_two**step_count
    weight_full = weight.astype(jnp.float32)
    direction = first_new / corr_one / (jnp.sqrt(second_new / corr_two) + adam_epsilon)
    updated = weight_full - learn_rate * (direction + weight_decay * weight_full)
    return (
        updated.astype(jnp.bfloat16),
        first_new.astype(jnp.bfloat16),
        second_new.astype(jnp.bfloat16),
    )


def block_ranks(hit):
    return jnp.cumsum(hit.astype(jnp.int32), axis=-1) - 1


def slot_onehot(hit, rank, capacity):
    slot_iota = jnp.arange(capacity, dtype=jnp.int32)
    return hit[..., None, :] & (rank[..., None, :] == slot_iota[:, None])


def on_device(
    grad_out, routes, router_probs, saved_hidden, down_weight, moment_one, moment_two, partner
):
    tok_rows, top_count = routes.shape
    width = grad_out.shape[1]
    axis_size = lax.axis_size("expert")
    me = lax.axis_index("expert")
    expert_count = partner.shape[0]
    capacity = 3 * tok_rows * top_count // (2 * expert_count)
    slot_count = capacity * axis_size

    weight = down_weight[0]
    weight_full = lax.all_gather(weight, "dp", axis=0, tiled=True)
    hidden = saved_hidden[0, 0]

    prob_sum = jnp.sum(router_probs, axis=1, keepdims=True)
    gate_share = router_probs / prob_sum
    gate_low = gate_share.astype(jnp.bfloat16)

    expert_iota = jnp.arange(expert_count, dtype=jnp.int32)
    local_hit = jnp.any(routes[:, :, None] == expert_iota[None, None, :], axis=1)
    local_rank = block_ranks(local_hit.T).T
    pair_rank = jnp.take_along_axis(local_rank, routes, axis=1)

    gather_bytes = axis_size * tok_rows * width * grad_out.dtype.itemsize
    if gather_bytes <= gather_limit_bytes:
        packed = jnp.concatenate([routes.astype(jnp.float32), router_probs], axis=1)
        packed_all = lax.all_gather(packed, "expert", axis=0, tiled=True)
        grad_all = lax.all_gather(grad_out, "expert", axis=0, tiled=True)
        routes_all = packed_all[:, :top_count].astype(jnp.int32)
        probs_all = packed_all[:, top_count:]
        gate_all = (probs_all / jnp.sum(probs_all, axis=1, keepdims=True)).astype(jnp.bfloat16)
        hit_k = routes_all == me
        hit = jnp.any(hit_k, axis=1).reshape(axis_size, tok_rows)
        gate_tok = jnp.sum(
            jnp.where(hit_k, gate_all.astype(jnp.float32), 0.0), axis=1
        ).reshape(axis_size, tok_rows)
        onehot = slot_onehot(hit, block_ranks(hit), capacity)
        dispatched = jnp.einsum(
            "sjt,std->sjd",
            onehot.astype(jnp.bfloat16),
            grad_all.reshape(axis_size, tok_rows, width),
            preferred_element_type=jnp.float32,
        ).astype(jnp.bfloat16)
        slot_gate = jnp.sum(
            jnp.where(onehot, gate_tok[:, None, :], 0.0), axis=2
        ).astype(jnp.bfloat16)
    else:
        gate_pair = jnp.sum(
            jnp.where(
                routes[:, :, None] == expert_iota[None, None, :],
                gate_low.astype(jnp.float32)[:, :, None],
                0.0,
            ),
            axis=1,
        )
        onehot = slot_onehot(local_hit.T, local_rank.T, capacity)
        send_rows = jnp.einsum(
            "ejt,td->ejd",
            onehot.astype(jnp.bfloat16),
            grad_out,
            preferred_element_type=jnp.float32,
        ).astype(jnp.bfloat16)
        send_gate = jnp.sum(jnp.where(onehot, gate_pair.T[:, None, :], 0.0), axis=2).astype(
            jnp.bfloat16
        )
        dispatched = lax.all_to_all(send_rows, "expert", split_axis=0, concat_axis=0, tiled=True)
        slot_gate = lax.all_to_all(send_gate, "expert", split_axis=0, concat_axis=0, tiled=True)

    dispatched = dispatched.reshape(slot_count, width)
    slot_gate = slot_gate.reshape(slot_count)
    scaled = slot_gate[:, None] * dispatched
    projected = lax.dot_general(
        dispatched,
        weight_full,
        (((1,), (1,)), ((), ())),
        preferred_element_type=jnp.float32,
    )
    products = jnp.sum(hidden.astype(jnp.float32) * projected, axis=1)
    grad_sum = lax.psum_scatter(
        lax.dot_general(
            hidden, scaled, (((0,), (0,)), ((), ())), preferred_element_type=jnp.float32
        ).astype(jnp.bfloat16),
        "dp",
        scatter_dimension=0,
        tiled=True,
    ).astype(jnp.float32)
    returned = lax.all_to_all(
        products.reshape(axis_size, capacity), "expert", split_axis=0, concat_axis=0, tiled=True
    )
    answer = returned.reshape(-1)[routes * capacity + pair_rank]
    gate_grad = (answer - jnp.sum(gate_share * answer, axis=1, keepdims=True)) / prob_sum

    outputs = jnp.stack(adam_update(weight, moment_one[0], moment_two[0], grad_sum))
    outputs, gate_grad = lax.optimization_barrier((outputs, gate_grad))

    mine = partner[me]
    levels = axis_size.bit_length() - 1
    which = jnp.int32(0)
    cases = [outputs]
    for level in range(levels):
        flip = 1 << level
        which = which + jnp.where(mine == (me ^ flip), level + 1, 0).astype(jnp.int32)
        cases.append(
            lax.ppermute(outputs, "expert", perm=[(i, i ^ flip) for i in range(axis_size)])
        )
    landed = lax.select_n(which, *cases)
    return (gate_grad, landed[0][None], landed[1][None], landed[2][None])


def solution(mesh):
    in_specs = (
        P(("dp", "expert"), None),
        P(("dp", "expert"), None),
        P(("dp", "expert"), None),
        P("expert", "dp", None, None),
        P("expert", "dp", None),
        P("expert", "dp", None),
        P("expert", "dp", None),
        P(),
    )
    out_specs = (
        P(("dp", "expert"), None),
        P("expert", "dp", None),
        P("expert", "dp", None),
        P("expert", "dp", None),
    )
    return jax.shard_map(
        on_device, mesh=mesh, in_specs=in_specs, out_specs=out_specs, check_vma=False
    )
```

```python
import jax
import jax.numpy as jnp
from jax import lax
from jax.sharding import PartitionSpec as P

beta_one = 0.9
beta_two = 0.95
learn_rate = 0.001
weight_decay = 0.1
adam_epsilon = 1e-08
step_count = 1000

gather_limit_bytes = 16 * 1024 * 1024


def adam_update(weight, moment_first, moment_second, grad_sum):
    first_new = beta_one * moment_first.astype(jnp.float32) + (1.0 - beta_one) * grad_sum
    second_new = (
        beta_two * moment_second.astype(jnp.float32) + (1.0 - beta_two) * grad_sum * grad_sum
    )
    corr_one = 1.0 - beta_one**step_count
    corr_two = 1.0 - beta_two**step_count
    weight_full = weight.astype(jnp.float32)
    direction = first_new / corr_one / (jnp.sqrt(second_new / corr_two) + adam_epsilon)
    updated = weight_full - learn_rate * (direction + weight_decay * weight_full)
    return (
        updated.astype(jnp.bfloat16),
        first_new.astype(jnp.bfloat16),
        second_new.astype(jnp.bfloat16),
    )


def block_ranks(hit):
    return jnp.cumsum(hit.astype(jnp.int32), axis=-1) - 1


def slot_onehot(hit, rank, capacity):
    slot_iota = jnp.arange(capacity, dtype=jnp.int32)
    return hit[..., None, :] & (rank[..., None, :] == slot_iota[:, None])


def on_device(
    grad_out, routes, router_probs, saved_hidden, down_weight, moment_one, moment_two, partner
):
    tok_rows, top_count = routes.shape
    width = grad_out.shape[1]
    axis_size = lax.axis_size("expert")
    me = lax.axis_index("expert")
    expert_count = partner.shape[0]
    capacity = 3 * tok_rows * top_count // (2 * expert_count)
    slot_count = capacity * axis_size

    weight = down_weight[0]
    weight_full = lax.all_gather(weight, "dp", axis=0, tiled=True)
    hidden = saved_hidden[0, 0]

    prob_sum = jnp.sum(router_probs, axis=1, keepdims=True)
    gate_share = router_probs / prob_sum
    gate_low = gate_share.astype(jnp.bfloat16)

    expert_iota = jnp.arange(expert_count, dtype=jnp.int32)
    local_hit = jnp.any(routes[:, :, None] == expert_iota[None, None, :], axis=1)
    local_rank = block_ranks(local_hit.T).T
    pair_rank = jnp.take_along_axis(local_rank, routes, axis=1)

    gather_bytes = axis_size * tok_rows * width * grad_out.dtype.itemsize
    if gather_bytes <= gather_limit_bytes:
        packed = jnp.concatenate([routes.astype(jnp.float32), router_probs], axis=1)
        packed_all = lax.all_gather(packed, "expert", axis=0, tiled=True)
        grad_all = lax.all_gather(grad_out, "expert", axis=0, tiled=True)
        routes_all = packed_all[:, :top_count].astype(jnp.int32)
        probs_all = packed_all[:, top_count:]
        gate_all = (probs_all / jnp.sum(probs_all, axis=1, keepdims=True)).astype(jnp.bfloat16)
        hit_k = routes_all == me
        hit = jnp.any(hit_k, axis=1).reshape(axis_size, tok_rows)
        gate_tok = jnp.sum(
            jnp.where(hit_k, gate_all.astype(jnp.float32), 0.0), axis=1
        ).reshape(axis_size, tok_rows)
        onehot = slot_onehot(hit, block_ranks(hit), capacity)
        dispatched = jnp.einsum(
            "sjt,std->sjd",
            onehot.astype(jnp.bfloat16),
            grad_all.reshape(axis_size, tok_rows, width),
            preferred_element_type=jnp.float32,
        ).astype(jnp.bfloat16)
        slot_gate = jnp.sum(
            jnp.where(onehot, gate_tok[:, None, :], 0.0), axis=2
        ).astype(jnp.bfloat16)
    else:
        gate_pair = jnp.sum(
            jnp.where(
                routes[:, :, None] == expert_iota[None, None, :],
                gate_low.astype(jnp.float32)[:, :, None],
                0.0,
            ),
            axis=1,
        )
        onehot = slot_onehot(local_hit.T, local_rank.T, capacity)
        send_rows = jnp.einsum(
            "ejt,td->ejd",
            onehot.astype(jnp.bfloat16),
            grad_out,
            preferred_element_type=jnp.float32,
        ).astype(jnp.bfloat16)
        send_gate = jnp.sum(jnp.where(onehot, gate_pair.T[:, None, :], 0.0), axis=2).astype(
            jnp.bfloat16
        )
        dispatched = lax.all_to_all(send_rows, "expert", split_axis=0, concat_axis=0, tiled=True)
        slot_gate = lax.all_to_all(send_gate, "expert", split_axis=0, concat_axis=0, tiled=True)

    dispatched = dispatched.reshape(slot_count, width)
    slot_gate = slot_gate.reshape(slot_count)
    scaled = slot_gate[:, None] * dispatched
    projected = lax.dot_general(
        dispatched,
        weight_full,
        (((1,), (1,)), ((), ())),
        preferred_element_type=jnp.float32,
    )
    products = jnp.sum(hidden.astype(jnp.float32) * projected, axis=1)
    grad_sum = lax.psum_scatter(
        lax.dot_general(
            hidden, scaled, (((0,), (0,)), ((), ())), preferred_element_type=jnp.float32
        ).astype(jnp.bfloat16),
        "dp",
        scatter_dimension=0,
        tiled=True,
    ).astype(jnp.float32)
    returned = lax.all_to_all(
        products.reshape(axis_size, capacity), "expert", split_axis=0, concat_axis=0, tiled=True
    )
    answer = returned.reshape(-1)[routes * capacity + pair_rank]
    gate_grad = (answer - jnp.sum(gate_share * answer, axis=1, keepdims=True)) / prob_sum

    outputs = jnp.stack(adam_update(weight, moment_one[0], moment_two[0], grad_sum))
    outputs, gate_grad = lax.optimization_barrier((outputs, gate_grad))

    mine = partner[me]
    levels = axis_size.bit_length() - 1
    device_iota = jnp.arange(expert_count, dtype=jnp.int32)
    which = jnp.int32(0)
    for level in range(levels):
        which = which + jnp.where(mine == (me ^ (1 << level)), level + 1, 0).astype(jnp.int32)

    def exchange(arrays, level):
        flip = 1 << level
        return lax.ppermute(arrays, "expert", perm=[(i, i ^ flip) for i in range(axis_size)])

    optional = list(range(max(levels - 2, 0), levels))
    cases = [outputs] + [exchange(outputs, level) for level in range(levels - len(optional))]
    if optional:
        choice = jnp.int32(0)
        for position, level in enumerate(optional):
            used = jnp.any(partner == (device_iota ^ (1 << level)))
            choice = choice + jnp.where(used, 1 << position, 0).astype(jnp.int32)

        def branch(mask):
            def run(arrays):
                return tuple(
                    exchange(arrays, level) if mask >> position & 1 else arrays
                    for position, level in enumerate(optional)
                )

            return run

        cases += list(lax.switch(choice, [branch(mask) for mask in range(1 << len(optional))], outputs))
    landed = lax.select_n(which, *cases)
    return (gate_grad, landed[0][None], landed[1][None], landed[2][None])


def solution(mesh):
    in_specs = (
        P(("dp", "expert"), None),
        P(("dp", "expert"), None),
        P(("dp", "expert"), None),
        P("expert", "dp", None, None),
        P("expert", "dp", None),
        P("expert", "dp", None),
        P("expert", "dp", None),
        P(),
    )
    out_specs = (
        P(("dp", "expert"), None),
        P("expert", "dp", None),
        P("expert", "dp", None),
        P("expert", "dp", None),
    )
    return jax.shard_map(
        on_device, mesh=mesh, in_specs=in_specs, out_specs=out_specs, check_vma=False
    )
```

```python
import jax
import jax.numpy as jnp
from jax import lax
from jax.sharding import PartitionSpec as P

beta_one = 0.9
beta_two = 0.95
learn_rate = 0.001
weight_decay = 0.1
adam_epsilon = 1e-08
step_count = 1000

gather_limit_bytes = 16 * 1024 * 1024


def adam_update(weight, moment_first, moment_second, grad_sum):
    first_new = beta_one * moment_first.astype(jnp.float32) + (1.0 - beta_one) * grad_sum
    second_new = (
        beta_two * moment_second.astype(jnp.float32) + (1.0 - beta_two) * grad_sum * grad_sum
    )
    corr_one = 1.0 - beta_one**step_count
    corr_two = 1.0 - beta_two**step_count
    weight_full = weight.astype(jnp.float32)
    direction = first_new / corr_one / (jnp.sqrt(second_new / corr_two) + adam_epsilon)
    updated = weight_full - learn_rate * (direction + weight_decay * weight_full)
    return (
        updated.astype(jnp.bfloat16),
        first_new.astype(jnp.bfloat16),
        second_new.astype(jnp.bfloat16),
    )


def block_ranks(hit):
    return jnp.cumsum(hit.astype(jnp.int32), axis=-1) - 1


def slot_onehot(hit, rank, capacity):
    slot_iota = jnp.arange(capacity, dtype=jnp.int32)
    return hit[..., None, :] & (rank[..., None, :] == slot_iota[:, None])


def on_device(
    grad_out, routes, router_probs, saved_hidden, down_weight, moment_one, moment_two, partner
):
    tok_rows, top_count = routes.shape
    width = grad_out.shape[1]
    axis_size = lax.axis_size("expert")
    me = lax.axis_index("expert")
    expert_count = partner.shape[0]
    capacity = 3 * tok_rows * top_count // (2 * expert_count)
    slot_count = capacity * axis_size

    weight = down_weight[0]
    weight_full = lax.all_gather(weight, "dp", axis=0, tiled=True)
    hidden = saved_hidden[0, 0]

    prob_sum = jnp.sum(router_probs, axis=1, keepdims=True)
    gate_share = router_probs / prob_sum
    gate_low = gate_share.astype(jnp.bfloat16)

    expert_iota = jnp.arange(expert_count, dtype=jnp.int32)
    local_hit = jnp.any(routes[:, :, None] == expert_iota[None, None, :], axis=1)
    local_rank = block_ranks(local_hit.T).T
    pair_rank = jnp.take_along_axis(local_rank, routes, axis=1)

    gather_bytes = axis_size * tok_rows * width * grad_out.dtype.itemsize
    if gather_bytes <= gather_limit_bytes:
        packed = jnp.concatenate([routes.astype(jnp.float32), router_probs], axis=1)
        packed_all = lax.all_gather(packed, "expert", axis=0, tiled=True)
        grad_all = lax.all_gather(grad_out, "expert", axis=0, tiled=True)
        routes_all = packed_all[:, :top_count].astype(jnp.int32)
        probs_all = packed_all[:, top_count:]
        gate_all = (probs_all / jnp.sum(probs_all, axis=1, keepdims=True)).astype(jnp.bfloat16)
        hit_k = routes_all == me
        hit = jnp.any(hit_k, axis=1).reshape(axis_size, tok_rows)
        gate_tok = jnp.sum(
            jnp.where(hit_k, gate_all.astype(jnp.float32), 0.0), axis=1
        ).reshape(axis_size, tok_rows)
        onehot = slot_onehot(hit, block_ranks(hit), capacity)
        dispatched = jnp.einsum(
            "sjt,std->sjd",
            onehot.astype(jnp.bfloat16),
            grad_all.reshape(axis_size, tok_rows, width),
            preferred_element_type=jnp.float32,
        ).astype(jnp.bfloat16)
        slot_gate = jnp.sum(
            jnp.where(onehot, gate_tok[:, None, :], 0.0), axis=2
        ).astype(jnp.bfloat16)
    else:
        gate_pair = jnp.sum(
            jnp.where(
                routes[:, :, None] == expert_iota[None, None, :],
                gate_low.astype(jnp.float32)[:, :, None],
                0.0,
            ),
            axis=1,
        )
        onehot = slot_onehot(local_hit.T, local_rank.T, capacity)
        send_rows = jnp.einsum(
            "ejt,td->ejd",
            onehot.astype(jnp.bfloat16),
            grad_out,
            preferred_element_type=jnp.float32,
        ).astype(jnp.bfloat16)
        send_gate = jnp.sum(jnp.where(onehot, gate_pair.T[:, None, :], 0.0), axis=2).astype(
            jnp.bfloat16
        )
        dispatched = lax.all_to_all(send_rows, "expert", split_axis=0, concat_axis=0, tiled=True)
        slot_gate = lax.all_to_all(send_gate, "expert", split_axis=0, concat_axis=0, tiled=True)

    dispatched = dispatched.reshape(slot_count, width)
    slot_gate = slot_gate.reshape(slot_count)
    scaled = slot_gate[:, None] * dispatched
    projected = lax.dot_general(
        dispatched,
        weight_full,
        (((1,), (1,)), ((), ())),
        preferred_element_type=jnp.float32,
    )
    products = jnp.sum(hidden.astype(jnp.float32) * projected, axis=1)
    grad_sum = lax.psum_scatter(
        lax.dot_general(
            hidden, scaled, (((0,), (0,)), ((), ())), preferred_element_type=jnp.float32
        ).astype(jnp.bfloat16),
        "dp",
        scatter_dimension=0,
        tiled=True,
    ).astype(jnp.float32)
    returned = lax.all_to_all(
        products.reshape(axis_size, capacity), "expert", split_axis=0, concat_axis=0, tiled=True
    )
    expert_rows = jnp.sum(
        jnp.where(
            (routes[:, :, None] == expert_iota)[..., None], returned[None, None, :, :], 0.0
        ),
        axis=2,
    )
    answer = jnp.sum(
        jnp.where(pair_rank[..., None] == jnp.arange(capacity), expert_rows, 0.0), axis=2
    )
    gate_grad = (answer - jnp.sum(gate_share * answer, axis=1, keepdims=True)) / prob_sum

    outputs = jnp.stack(adam_update(weight, moment_one[0], moment_two[0], grad_sum))
    outputs, gate_grad = lax.optimization_barrier((outputs, gate_grad))

    mine = partner[me]
    levels = axis_size.bit_length() - 1
    device_iota = jnp.arange(expert_count, dtype=jnp.int32)
    which = jnp.int32(0)
    for level in range(levels):
        which = which + jnp.where(mine == (me ^ (1 << level)), level + 1, 0).astype(jnp.int32)

    def exchange(arrays, level):
        flip = 1 << level
        return lax.ppermute(arrays, "expert", perm=[(i, i ^ flip) for i in range(axis_size)])

    optional = list(range(max(levels - 2, 0), levels))
    fixed = list(range(levels - len(optional)))
    cases = [outputs] + [exchange(outputs, level) for level in fixed]
    if optional:
        choice = jnp.int32(0)
        for position, level in enumerate(optional):
            used = jnp.any(partner == (device_iota ^ (1 << level)))
            choice = choice + jnp.where(used, 1 << position, 0).astype(jnp.int32)

        def branch(mask):
            def run(arrays):
                chosen = [level for position, level in enumerate(optional) if mask >> position & 1]
                picks = [arrays] + [exchange(arrays, level) for level in chosen]
                index = jnp.int32(0)
                for position, level in enumerate(chosen):
                    index = index + jnp.where(which == level + 1, position + 1, 0).astype(
                        jnp.int32
                    )
                return lax.select_n(index, *picks) if chosen else arrays

            return run

        cases[0] = lax.switch(choice, [branch(mask) for mask in range(1 << len(optional))], outputs)
    top_index = jnp.where(which <= len(fixed), which, 0)
    landed = lax.select_n(top_index, *cases)
    return (gate_grad, landed[0][None], landed[1][None], landed[2][None])


def solution(mesh):
    in_specs = (
        P(("dp", "expert"), None),
        P(("dp", "expert"), None),
        P(("dp", "expert"), None),
        P("expert", "dp", None, None),
        P("expert", "dp", None),
        P("expert", "dp", None),
        P("expert", "dp", None),
        P(),
    )
    out_specs = (
        P(("dp", "expert"), None),
        P("expert", "dp", None),
        P("expert", "dp", None),
        P("expert", "dp", None),
    )
    return jax.shard_map(
        on_device, mesh=mesh, in_specs=in_specs, out_specs=out_specs, check_vma=False
    )
```

```python
import jax
import jax.numpy as jnp
from jax import lax
from jax.sharding import PartitionSpec as P

beta_one = 0.9
beta_two = 0.95
learn_rate = 0.001
weight_decay = 0.1
adam_epsilon = 1e-08
step_count = 1000

gather_limit_bytes = 16 * 1024 * 1024


def adam_update(weight, moment_first, moment_second, grad_sum):
    first_new = beta_one * moment_first.astype(jnp.float32) + (1.0 - beta_one) * grad_sum
    second_new = (
        beta_two * moment_second.astype(jnp.float32) + (1.0 - beta_two) * grad_sum * grad_sum
    )
    corr_one = 1.0 - beta_one**step_count
    corr_two = 1.0 - beta_two**step_count
    weight_full = weight.astype(jnp.float32)
    direction = first_new / corr_one / (jnp.sqrt(second_new / corr_two) + adam_epsilon)
    updated = weight_full - learn_rate * (direction + weight_decay * weight_full)
    return (
        updated.astype(jnp.bfloat16),
        first_new.astype(jnp.bfloat16),
        second_new.astype(jnp.bfloat16),
    )


def block_ranks(hit):
    return jnp.cumsum(hit.astype(jnp.int32), axis=-1) - 1


def slot_onehot(hit, rank, capacity):
    slot_iota = jnp.arange(capacity, dtype=jnp.int32)
    return hit[..., None, :] & (rank[..., None, :] == slot_iota[:, None])


def on_device(
    grad_out, routes, router_probs, saved_hidden, down_weight, moment_one, moment_two, partner
):
    tok_rows, top_count = routes.shape
    width = grad_out.shape[1]
    axis_size = lax.axis_size("expert")
    me = lax.axis_index("expert")
    expert_count = partner.shape[0]
    capacity = 3 * tok_rows * top_count // (2 * expert_count)
    slot_count = capacity * axis_size

    weight = down_weight[0]
    weight_full = lax.all_gather(weight, "dp", axis=0, tiled=True)
    hidden = saved_hidden[0, 0]

    prob_sum = jnp.sum(router_probs, axis=1, keepdims=True)
    gate_share = router_probs / prob_sum
    gate_low = gate_share.astype(jnp.bfloat16)

    expert_iota = jnp.arange(expert_count, dtype=jnp.int32)
    local_hit = jnp.any(routes[:, :, None] == expert_iota[None, None, :], axis=1)
    local_rank = block_ranks(local_hit.T).T
    pair_rank = jnp.take_along_axis(local_rank, routes, axis=1)

    gather_bytes = axis_size * tok_rows * width * grad_out.dtype.itemsize
    if gather_bytes <= gather_limit_bytes:
        packed = jnp.concatenate([routes.astype(jnp.float32), router_probs], axis=1)
        packed_all = lax.all_gather(packed, "expert", axis=0, tiled=True)
        grad_all = lax.all_gather(grad_out, "expert", axis=0, tiled=True)
        routes_all = packed_all[:, :top_count].astype(jnp.int32)
        probs_all = packed_all[:, top_count:]
        gate_all = (probs_all / jnp.sum(probs_all, axis=1, keepdims=True)).astype(jnp.bfloat16)
        hit_k = routes_all == me
        hit = jnp.any(hit_k, axis=1).reshape(axis_size, tok_rows)
        gate_tok = jnp.sum(
            jnp.where(hit_k, gate_all.astype(jnp.float32), 0.0), axis=1
        ).reshape(axis_size, tok_rows)
        onehot = slot_onehot(hit, block_ranks(hit), capacity)
        dispatched = jnp.einsum(
            "sjt,std->sjd",
            onehot.astype(jnp.bfloat16),
            grad_all.reshape(axis_size, tok_rows, width),
            preferred_element_type=jnp.float32,
        ).astype(jnp.bfloat16)
        slot_gate = jnp.sum(
            jnp.where(onehot, gate_tok[:, None, :], 0.0), axis=2
        ).astype(jnp.bfloat16)
    else:
        gate_pair = jnp.sum(
            jnp.where(
                routes[:, :, None] == expert_iota[None, None, :],
                gate_low.astype(jnp.float32)[:, :, None],
                0.0,
            ),
            axis=1,
        )
        onehot = slot_onehot(local_hit.T, local_rank.T, capacity)
        send_rows = jnp.einsum(
            "ejt,td->ejd",
            onehot.astype(jnp.bfloat16),
            grad_out,
            preferred_element_type=jnp.float32,
        ).astype(jnp.bfloat16)
        send_gate = jnp.sum(jnp.where(onehot, gate_pair.T[:, None, :], 0.0), axis=2).astype(
            jnp.bfloat16
        )
        dispatched = lax.all_to_all(send_rows, "expert", split_axis=0, concat_axis=0, tiled=True)
        slot_gate = lax.all_to_all(send_gate, "expert", split_axis=0, concat_axis=0, tiled=True)

    dispatched = dispatched.reshape(slot_count, width)
    slot_gate = slot_gate.reshape(slot_count)
    scaled = slot_gate[:, None] * dispatched
    projected = lax.dot_general(
        dispatched,
        weight_full,
        (((1,), (1,)), ((), ())),
        preferred_element_type=jnp.float32,
    )
    products = jnp.sum(hidden.astype(jnp.float32) * projected, axis=1)
    grad_sum = lax.psum_scatter(
        lax.dot_general(
            hidden, scaled, (((0,), (0,)), ((), ())), preferred_element_type=jnp.float32
        ).astype(jnp.bfloat16),
        "dp",
        scatter_dimension=0,
        tiled=True,
    ).astype(jnp.float32)
    returned = lax.all_to_all(
        products.reshape(axis_size, capacity), "expert", split_axis=0, concat_axis=0, tiled=True
    )
    expert_rows = jnp.sum(
        jnp.where(
            (routes[:, :, None] == expert_iota)[..., None], returned[None, None, :, :], 0.0
        ),
        axis=2,
    )
    answer = jnp.sum(
        jnp.where(pair_rank[..., None] == jnp.arange(capacity), expert_rows, 0.0), axis=2
    )
    gate_grad = (answer - jnp.sum(gate_share * answer, axis=1, keepdims=True)) / prob_sum

    outputs = jnp.stack(adam_update(weight, moment_one[0], moment_two[0], grad_sum))
    outputs, gate_grad = lax.optimization_barrier((outputs, gate_grad))

    mine = partner[me]
    levels = axis_size.bit_length() - 1
    device_iota = jnp.arange(expert_count, dtype=jnp.int32)
    which = jnp.int32(0)
    for level in range(levels):
        which = which + jnp.where(mine == (me ^ (1 << level)), level + 1, 0).astype(jnp.int32)

    def exchange(arrays, level, pairs=None):
        flip = 1 << level
        pairs = range(axis_size) if pairs is None else pairs
        return lax.ppermute(arrays, "expert", perm=[(i, i ^ flip) for i in pairs])

    optional = list(range(max(levels - 2, 0), levels))
    fixed = list(range(levels - len(optional)))
    cases = [outputs] + [exchange(outputs, level) for level in fixed]
    if optional:
        classes = []
        for level in optional:
            other = [bit for bit in optional if bit != level]
            for value in range(2 if other else 1):
                members = [
                    i for i in range(axis_size) if not other or (i >> other[0] & 1) == value
                ]
                classes.append((level, members))
        choice = jnp.int32(0)
        for position, (level, members) in enumerate(classes):
            member_iota = jnp.asarray(members, dtype=jnp.int32)
            used = jnp.any(partner[member_iota] == (member_iota ^ (1 << level)))
            choice = choice + jnp.where(used, 1 << position, 0).astype(jnp.int32)
        member_of = [
            jnp.any(jnp.asarray(members, dtype=jnp.int32) == me) for _, members in classes
        ]

        def branch(mask):
            def run(arrays):
                picks = [arrays]
                index = jnp.int32(0)
                for position, (level, members) in enumerate(classes):
                    if mask >> position & 1:
                        picks.append(exchange(arrays, level, members))
                        hit = (which == level + 1) & member_of[position]
                        index = index + jnp.where(hit, len(picks) - 1, 0).astype(jnp.int32)
                return lax.select_n(index, *picks) if len(picks) > 1 else arrays

            return run

        cases[0] = lax.switch(choice, [branch(mask) for mask in range(1 << len(classes))], outputs)
    top_index = jnp.where(which <= len(fixed), which, 0)
    landed = lax.select_n(top_index, *cases)
    return (gate_grad, landed[0][None], landed[1][None], landed[2][None])


def solution(mesh):
    in_specs = (
        P(("dp", "expert"), None),
        P(("dp", "expert"), None),
        P(("dp", "expert"), None),
        P("expert", "dp", None, None),
        P("expert", "dp", None),
        P("expert", "dp", None),
        P("expert", "dp", None),
        P(),
    )
    out_specs = (
        P(("dp", "expert"), None),
        P("expert", "dp", None),
        P("expert", "dp", None),
        P("expert", "dp", None),
    )
    return jax.shard_map(
        on_device, mesh=mesh, in_specs=in_specs, out_specs=out_specs, check_vma=False
    )
```

```python
import jax
import jax.numpy as jnp
from jax import lax
from jax.sharding import PartitionSpec as P

beta_one = 0.9
beta_two = 0.95
learn_rate = 0.001
weight_decay = 0.1
adam_epsilon = 1e-08
step_count = 1000

gather_limit_bytes = 16 * 1024 * 1024


def adam_update(weight, moment_first, moment_second, grad_sum):
    first_new = beta_one * moment_first.astype(jnp.float32) + (1.0 - beta_one) * grad_sum
    second_new = (
        beta_two * moment_second.astype(jnp.float32) + (1.0 - beta_two) * grad_sum * grad_sum
    )
    corr_one = 1.0 - beta_one**step_count
    corr_two = 1.0 - beta_two**step_count
    weight_full = weight.astype(jnp.float32)
    direction = first_new / corr_one / (jnp.sqrt(second_new / corr_two) + adam_epsilon)
    updated = weight_full - learn_rate * (direction + weight_decay * weight_full)
    return (
        updated.astype(jnp.bfloat16),
        first_new.astype(jnp.bfloat16),
        second_new.astype(jnp.bfloat16),
    )


def block_ranks(hit):
    return jnp.cumsum(hit.astype(jnp.int32), axis=-1) - 1


def slot_onehot(hit, rank, capacity):
    slot_iota = jnp.arange(capacity, dtype=jnp.int32)
    return hit[..., None, :] & (rank[..., None, :] == slot_iota[:, None])


def on_device(
    grad_out, routes, router_probs, saved_hidden, down_weight, moment_one, moment_two, partner
):
    tok_rows, top_count = routes.shape
    width = grad_out.shape[1]
    axis_size = lax.axis_size("expert")
    me = lax.axis_index("expert")
    expert_count = partner.shape[0]
    capacity = 3 * tok_rows * top_count // (2 * expert_count)
    slot_count = capacity * axis_size

    weight = down_weight[0]
    weight_full = lax.all_gather(weight, "dp", axis=0, tiled=True)

    mine = partner[me]
    levels = axis_size.bit_length() - 1
    device_iota = jnp.arange(expert_count, dtype=jnp.int32)
    which = jnp.int32(0)
    for level in range(levels):
        which = which + jnp.where(mine == (me ^ (1 << level)), level + 1, 0).astype(jnp.int32)

    def exchange(arrays, level):
        flip = 1 << level
        return lax.ppermute(arrays, "expert", perm=[(i, i ^ flip) for i in range(axis_size)])

    optional = list(range(max(levels - 2, 0), levels))
    fixed = list(range(levels - len(optional)))
    inputs = jnp.stack([weight, moment_one[0], moment_two[0]])
    early = [exchange(inputs, level) for level in fixed]
    fixed_index = jnp.where(which <= len(fixed), which, 0)
    hidden = saved_hidden[0, 0]

    prob_sum = jnp.sum(router_probs, axis=1, keepdims=True)
    gate_share = router_probs / prob_sum
    gate_low = gate_share.astype(jnp.bfloat16)

    expert_iota = jnp.arange(expert_count, dtype=jnp.int32)
    local_hit = jnp.any(routes[:, :, None] == expert_iota[None, None, :], axis=1)
    local_rank = block_ranks(local_hit.T).T
    pair_rank = jnp.take_along_axis(local_rank, routes, axis=1)

    gather_bytes = axis_size * tok_rows * width * grad_out.dtype.itemsize
    if gather_bytes <= gather_limit_bytes:
        packed = jnp.concatenate([routes.astype(jnp.float32), router_probs], axis=1)
        packed_all = lax.all_gather(packed, "expert", axis=0, tiled=True)
        grad_all = lax.all_gather(grad_out, "expert", axis=0, tiled=True)
        routes_all = packed_all[:, :top_count].astype(jnp.int32)
        probs_all = packed_all[:, top_count:]
        gate_all = (probs_all / jnp.sum(probs_all, axis=1, keepdims=True)).astype(jnp.bfloat16)
        hit_k = routes_all == me
        hit = jnp.any(hit_k, axis=1).reshape(axis_size, tok_rows)
        gate_tok = jnp.sum(
            jnp.where(hit_k, gate_all.astype(jnp.float32), 0.0), axis=1
        ).reshape(axis_size, tok_rows)
        onehot = slot_onehot(hit, block_ranks(hit), capacity)
        dispatched = jnp.einsum(
            "sjt,std->sjd",
            onehot.astype(jnp.bfloat16),
            grad_all.reshape(axis_size, tok_rows, width),
            preferred_element_type=jnp.float32,
        ).astype(jnp.bfloat16)
        slot_gate = jnp.sum(
            jnp.where(onehot, gate_tok[:, None, :], 0.0), axis=2
        ).astype(jnp.bfloat16)
    else:
        gate_pair = jnp.sum(
            jnp.where(
                routes[:, :, None] == expert_iota[None, None, :],
                gate_low.astype(jnp.float32)[:, :, None],
                0.0,
            ),
            axis=1,
        )
        onehot = slot_onehot(local_hit.T, local_rank.T, capacity)
        send_rows = jnp.einsum(
            "ejt,td->ejd",
            onehot.astype(jnp.bfloat16),
            grad_out,
            preferred_element_type=jnp.float32,
        ).astype(jnp.bfloat16)
        send_gate = jnp.sum(jnp.where(onehot, gate_pair.T[:, None, :], 0.0), axis=2).astype(
            jnp.bfloat16
        )
        dispatched = lax.all_to_all(send_rows, "expert", split_axis=0, concat_axis=0, tiled=True)
        slot_gate = lax.all_to_all(send_gate, "expert", split_axis=0, concat_axis=0, tiled=True)

    dispatched = dispatched.reshape(slot_count, width)
    dispatched, early = lax.optimization_barrier((dispatched, early))
    slot_gate = slot_gate.reshape(slot_count)
    scaled = slot_gate[:, None] * dispatched
    projected = lax.dot_general(
        dispatched,
        weight_full,
        (((1,), (1,)), ((), ())),
        preferred_element_type=jnp.float32,
    )
    products = jnp.sum(hidden.astype(jnp.float32) * projected, axis=1)
    grad_sum = lax.psum_scatter(
        lax.dot_general(
            hidden, scaled, (((0,), (0,)), ((), ())), preferred_element_type=jnp.float32
        ).astype(jnp.bfloat16),
        "dp",
        scatter_dimension=0,
        tiled=True,
    )
    returned = lax.all_to_all(
        products.reshape(axis_size, capacity), "expert", split_axis=0, concat_axis=0, tiled=True
    )
    expert_rows = jnp.sum(
        jnp.where(
            (routes[:, :, None] == expert_iota)[..., None], returned[None, None, :, :], 0.0
        ),
        axis=2,
    )
    answer = jnp.sum(
        jnp.where(pair_rank[..., None] == jnp.arange(capacity), expert_rows, 0.0), axis=2
    )
    gate_grad = (answer - jnp.sum(gate_share * answer, axis=1, keepdims=True)) / prob_sum

    late = [exchange(grad_sum, level) for level in fixed]
    chosen = lax.select_n(fixed_index, inputs, *early)
    chosen_grad = lax.select_n(fixed_index, grad_sum, *late)
    outputs = jnp.stack(
        adam_update(chosen[0], chosen[1], chosen[2], chosen_grad.astype(jnp.float32))
    )
    outputs, gate_grad = lax.optimization_barrier((outputs, gate_grad))

    cases = [outputs]
    if optional:
        choice = jnp.int32(0)
        for position, level in enumerate(optional):
            used = jnp.any(partner == (device_iota ^ (1 << level)))
            choice = choice + jnp.where(used, 1 << position, 0).astype(jnp.int32)

        def branch(mask):
            def run(arrays):
                chosen = [level for position, level in enumerate(optional) if mask >> position & 1]
                picks = [arrays] + [exchange(arrays, level) for level in chosen]
                index = jnp.int32(0)
                for position, level in enumerate(chosen):
                    index = index + jnp.where(which == level + 1, position + 1, 0).astype(
                        jnp.int32
                    )
                return lax.select_n(index, *picks) if chosen else arrays

            return run

        cases[0] = lax.switch(choice, [branch(mask) for mask in range(1 << len(optional))], outputs)
    landed = cases[0]
    return (gate_grad, landed[0][None], landed[1][None], landed[2][None])


def solution(mesh):
    in_specs = (
        P(("dp", "expert"), None),
        P(("dp", "expert"), None),
        P(("dp", "expert"), None),
        P("expert", "dp", None, None),
        P("expert", "dp", None),
        P("expert", "dp", None),
        P("expert", "dp", None),
        P(),
    )
    out_specs = (
        P(("dp", "expert"), None),
        P("expert", "dp", None),
        P("expert", "dp", None),
        P("expert", "dp", None),
    )
    return jax.shard_map(
        on_device, mesh=mesh, in_specs=in_specs, out_specs=out_specs, check_vma=False
    )
```

```python
import jax
import jax.numpy as jnp
from jax import lax
from jax.sharding import PartitionSpec as P

beta_one = 0.9
beta_two = 0.95
learn_rate = 0.001
weight_decay = 0.1
adam_epsilon = 1e-08
step_count = 1000

gather_limit_bytes = 16 * 1024 * 1024


def adam_update(weight, moment_first, moment_second, grad_sum):
    first_new = beta_one * moment_first.astype(jnp.float32) + (1.0 - beta_one) * grad_sum
    second_new = (
        beta_two * moment_second.astype(jnp.float32) + (1.0 - beta_two) * grad_sum * grad_sum
    )
    corr_one = 1.0 - beta_one**step_count
    corr_two = 1.0 - beta_two**step_count
    weight_full = weight.astype(jnp.float32)
    direction = first_new / corr_one / (jnp.sqrt(second_new / corr_two) + adam_epsilon)
    updated = weight_full - learn_rate * (direction + weight_decay * weight_full)
    return (
        updated.astype(jnp.bfloat16),
        first_new.astype(jnp.bfloat16),
        second_new.astype(jnp.bfloat16),
    )


def block_ranks(hit):
    return jnp.cumsum(hit.astype(jnp.int32), axis=-1) - 1


def slot_onehot(hit, rank, capacity):
    slot_iota = jnp.arange(capacity, dtype=jnp.int32)
    return hit[..., None, :] & (rank[..., None, :] == slot_iota[:, None])


def on_device(
    grad_out, routes, router_probs, saved_hidden, down_weight, moment_one, moment_two, partner
):
    tok_rows, top_count = routes.shape
    width = grad_out.shape[1]
    axis_size = lax.axis_size("expert")
    me = lax.axis_index("expert")
    expert_count = partner.shape[0]
    capacity = 3 * tok_rows * top_count // (2 * expert_count)
    slot_count = capacity * axis_size

    weight = down_weight[0]
    weight_full = lax.all_gather(weight, "dp", axis=0, tiled=True)
    hidden = saved_hidden[0, 0]

    prob_sum = jnp.sum(router_probs, axis=1, keepdims=True)
    gate_share = router_probs / prob_sum
    gate_low = gate_share.astype(jnp.bfloat16)

    expert_iota = jnp.arange(expert_count, dtype=jnp.int32)
    local_hit = jnp.any(routes[:, :, None] == expert_iota[None, None, :], axis=1)
    local_rank = block_ranks(local_hit.T).T
    pair_rank = jnp.take_along_axis(local_rank, routes, axis=1)

    gather_bytes = axis_size * tok_rows * width * grad_out.dtype.itemsize
    if gather_bytes <= gather_limit_bytes:
        packed = jnp.concatenate([routes.astype(jnp.float32), router_probs], axis=1)
        packed_all = lax.all_gather(packed, "expert", axis=0, tiled=True)
        grad_all = lax.all_gather(grad_out, "expert", axis=0, tiled=True)
        routes_all = packed_all[:, :top_count].astype(jnp.int32)
        probs_all = packed_all[:, top_count:]
        gate_all = (probs_all / jnp.sum(probs_all, axis=1, keepdims=True)).astype(jnp.bfloat16)
        hit_k = routes_all == me
        hit = jnp.any(hit_k, axis=1).reshape(axis_size, tok_rows)
        gate_tok = jnp.sum(
            jnp.where(hit_k, gate_all.astype(jnp.float32), 0.0), axis=1
        ).reshape(axis_size, tok_rows)
        onehot = slot_onehot(hit, block_ranks(hit), capacity)
        dispatched = jnp.einsum(
            "sjt,std->sjd",
            onehot.astype(jnp.bfloat16),
            grad_all.reshape(axis_size, tok_rows, width),
            preferred_element_type=jnp.float32,
        ).astype(jnp.bfloat16)
        slot_gate = jnp.sum(
            jnp.where(onehot, gate_tok[:, None, :], 0.0), axis=2
        ).astype(jnp.bfloat16)
    else:
        gate_pair = jnp.sum(
            jnp.where(
                routes[:, :, None] == expert_iota[None, None, :],
                gate_low.astype(jnp.float32)[:, :, None],
                0.0,
            ),
            axis=1,
        )
        onehot = slot_onehot(local_hit.T, local_rank.T, capacity)
        send_rows = jnp.einsum(
            "ejt,td->ejd",
            onehot.astype(jnp.bfloat16),
            grad_out,
            preferred_element_type=jnp.float32,
        ).astype(jnp.bfloat16)
        send_gate = jnp.sum(jnp.where(onehot, gate_pair.T[:, None, :], 0.0), axis=2).astype(
            jnp.bfloat16
        )
        dispatched = lax.all_to_all(send_rows, "expert", split_axis=0, concat_axis=0, tiled=True)
        slot_gate = lax.all_to_all(send_gate, "expert", split_axis=0, concat_axis=0, tiled=True)

    dispatched = dispatched.reshape(slot_count, width)
    slot_gate = slot_gate.reshape(slot_count)
    scaled = slot_gate[:, None] * dispatched
    projected = lax.dot_general(
        dispatched,
        weight_full,
        (((1,), (1,)), ((), ())),
        preferred_element_type=jnp.float32,
    )
    products = jnp.sum(hidden.astype(jnp.float32) * projected, axis=1)
    grad_sum = lax.psum_scatter(
        lax.dot_general(
            hidden, scaled, (((0,), (0,)), ((), ())), preferred_element_type=jnp.float32
        ).astype(jnp.bfloat16),
        "dp",
        scatter_dimension=0,
        tiled=True,
    ).astype(jnp.float32)
    returned = lax.all_to_all(
        products.reshape(axis_size, capacity), "expert", split_axis=0, concat_axis=0, tiled=True
    )
    expert_rows = jnp.sum(
        jnp.where(
            (routes[:, :, None] == expert_iota)[..., None], returned[None, None, :, :], 0.0
        ),
        axis=2,
    )
    answer = jnp.sum(
        jnp.where(pair_rank[..., None] == jnp.arange(capacity), expert_rows, 0.0), axis=2
    )
    gate_grad = (answer - jnp.sum(gate_share * answer, axis=1, keepdims=True)) / prob_sum

    outputs = jnp.stack(adam_update(weight, moment_one[0], moment_two[0], grad_sum))
    outputs, gate_grad = lax.optimization_barrier((outputs, gate_grad))

    mine = partner[me]
    levels = axis_size.bit_length() - 1
    device_iota = jnp.arange(expert_count, dtype=jnp.int32)
    which = jnp.int32(0)
    for level in range(levels):
        which = which + jnp.where(mine == (me ^ (1 << level)), level + 1, 0).astype(jnp.int32)

    def exchange(arrays, level, pairs=None):
        flip = 1 << level
        pairs = range(axis_size) if pairs is None else pairs
        return lax.ppermute(arrays, "expert", perm=[(i, i ^ flip) for i in pairs])

    optional = list(range(max(levels - 2, 0), levels))
    fixed = list(range(levels - len(optional)))
    cases = [outputs] + [exchange(outputs, level) for level in fixed]
    if optional:
        units = [(level, list(range(axis_size))) for level in optional[:-1]]
        top = optional[-1]
        other = optional[0] if len(optional) > 1 else None
        for value in range(2 if other is not None else 1):
            members = [i for i in range(axis_size) if other is None or (i >> other & 1) == value]
            units.append((top, members))
        choice = jnp.int32(0)
        member_of = []
        for position, (level, members) in enumerate(units):
            member_iota = jnp.asarray(members, dtype=jnp.int32)
            used = jnp.any(partner[member_iota] == (member_iota ^ (1 << level)))
            choice = choice + jnp.where(used, 1 << position, 0).astype(jnp.int32)
            member_of.append(jnp.any(member_iota == me))

        def branch(mask):
            def run(arrays):
                picks = [arrays]
                index = jnp.int32(0)
                for position, (level, members) in enumerate(units):
                    if mask >> position & 1:
                        picks.append(exchange(arrays, level, members))
                        hit = (which == level + 1) & member_of[position]
                        index = index + jnp.where(hit, len(picks) - 1, 0).astype(jnp.int32)
                return lax.select_n(index, *picks) if len(picks) > 1 else arrays

            return run

        cases[0] = lax.switch(choice, [branch(mask) for mask in range(1 << len(units))], outputs)
    top_index = jnp.where(which <= len(fixed), which, 0)
    landed = lax.select_n(top_index, *cases)
    return (gate_grad, landed[0][None], landed[1][None], landed[2][None])


def solution(mesh):
    in_specs = (
        P(("dp", "expert"), None),
        P(("dp", "expert"), None),
        P(("dp", "expert"), None),
        P("expert", "dp", None, None),
        P("expert", "dp", None),
        P("expert", "dp", None),
        P("expert", "dp", None),
        P(),
    )
    out_specs = (
        P(("dp", "expert"), None),
        P("expert", "dp", None),
        P("expert", "dp", None),
        P("expert", "dp", None),
    )
    return jax.shard_map(
        on_device, mesh=mesh, in_specs=in_specs, out_specs=out_specs, check_vma=False
    )
```

```python
import jax
import jax.numpy as jnp
from jax import lax
from jax.sharding import PartitionSpec as P
from jax.experimental.layout import Layout, with_layout_constraint

beta_one = 0.9
beta_two = 0.95
learn_rate = 0.001
weight_decay = 0.1
adam_epsilon = 1e-08
step_count = 1000

gather_limit_bytes = 16 * 1024 * 1024


def adam_update(weight, moment_first, moment_second, grad_sum):
    first_new = beta_one * moment_first.astype(jnp.float32) + (1.0 - beta_one) * grad_sum
    second_new = (
        beta_two * moment_second.astype(jnp.float32) + (1.0 - beta_two) * grad_sum * grad_sum
    )
    corr_one = 1.0 - beta_one**step_count
    corr_two = 1.0 - beta_two**step_count
    weight_full = weight.astype(jnp.float32)
    direction = first_new / corr_one / (jnp.sqrt(second_new / corr_two) + adam_epsilon)
    updated = weight_full - learn_rate * (direction + weight_decay * weight_full)
    return (
        updated.astype(jnp.bfloat16),
        first_new.astype(jnp.bfloat16),
        second_new.astype(jnp.bfloat16),
    )


def block_ranks(hit):
    return jnp.cumsum(hit.astype(jnp.int32), axis=-1) - 1


def slot_onehot(hit, rank, capacity):
    slot_iota = jnp.arange(capacity, dtype=jnp.int32)
    return hit[..., None, :] & (rank[..., None, :] == slot_iota[:, None])


def on_device(
    grad_out, routes, router_probs, saved_hidden, down_weight, moment_one, moment_two, partner
):
    tok_rows, top_count = routes.shape
    width = grad_out.shape[1]
    axis_size = lax.axis_size("expert")
    me = lax.axis_index("expert")
    expert_count = partner.shape[0]
    capacity = 3 * tok_rows * top_count // (2 * expert_count)
    slot_count = capacity * axis_size

    weight = down_weight[0]
    weight_full = lax.all_gather(weight, "dp", axis=0, tiled=True)
    hidden = saved_hidden[0, 0]

    prob_sum = jnp.sum(router_probs, axis=1, keepdims=True)
    gate_share = router_probs / prob_sum
    gate_low = gate_share.astype(jnp.bfloat16)

    expert_iota = jnp.arange(expert_count, dtype=jnp.int32)
    local_hit = jnp.any(routes[:, :, None] == expert_iota[None, None, :], axis=1)
    local_rank = block_ranks(local_hit.T).T
    pair_rank = jnp.take_along_axis(local_rank, routes, axis=1)

    gather_bytes = axis_size * tok_rows * width * grad_out.dtype.itemsize
    if gather_bytes <= gather_limit_bytes:
        packed = jnp.concatenate([routes.astype(jnp.float32), router_probs], axis=1)
        packed_all = lax.all_gather(packed, "expert", axis=0, tiled=True)
        grad_all = lax.all_gather(grad_out, "expert", axis=0, tiled=True)
        routes_all = packed_all[:, :top_count].astype(jnp.int32)
        probs_all = packed_all[:, top_count:]
        gate_all = (probs_all / jnp.sum(probs_all, axis=1, keepdims=True)).astype(jnp.bfloat16)
        hit_k = routes_all == me
        hit = jnp.any(hit_k, axis=1).reshape(axis_size, tok_rows)
        gate_tok = jnp.sum(
            jnp.where(hit_k, gate_all.astype(jnp.float32), 0.0), axis=1
        ).reshape(axis_size, tok_rows)
        onehot = slot_onehot(hit, block_ranks(hit), capacity)
        dispatched = jnp.einsum(
            "sjt,std->sjd",
            onehot.astype(jnp.bfloat16),
            grad_all.reshape(axis_size, tok_rows, width),
            preferred_element_type=jnp.float32,
        ).astype(jnp.bfloat16)
        slot_gate = jnp.sum(
            jnp.where(onehot, gate_tok[:, None, :], 0.0), axis=2
        ).astype(jnp.bfloat16)
    else:
        gate_pair = jnp.sum(
            jnp.where(
                routes[:, :, None] == expert_iota[None, None, :],
                gate_low.astype(jnp.float32)[:, :, None],
                0.0,
            ),
            axis=1,
        )
        onehot = slot_onehot(local_hit.T, local_rank.T, capacity)
        send_rows = jnp.einsum(
            "ejt,td->ejd",
            onehot.astype(jnp.bfloat16),
            grad_out,
            preferred_element_type=jnp.float32,
        ).astype(jnp.bfloat16)
        send_gate = jnp.sum(jnp.where(onehot, gate_pair.T[:, None, :], 0.0), axis=2).astype(
            jnp.bfloat16
        )
        dispatched = lax.all_to_all(send_rows, "expert", split_axis=0, concat_axis=0, tiled=True)
        slot_gate = lax.all_to_all(send_gate, "expert", split_axis=0, concat_axis=0, tiled=True)

    dispatched = dispatched.reshape(slot_count, width)
    slot_gate = slot_gate.reshape(slot_count)
    scaled = slot_gate[:, None] * dispatched
    projected = lax.dot_general(
        dispatched,
        weight_full,
        (((1,), (1,)), ((), ())),
        preferred_element_type=jnp.float32,
    )
    products = jnp.sum(hidden.astype(jnp.float32) * projected, axis=1)
    grad_full = lax.dot_general(
        hidden, scaled, (((0,), (0,)), ((), ())), preferred_element_type=jnp.float32
    ).astype(jnp.bfloat16)
    grad_full = with_layout_constraint(grad_full, Layout(major_to_minor=(0, 1)))
    grad_sum = lax.psum_scatter(
        grad_full,
        "dp",
        scatter_dimension=0,
        tiled=True,
    ).astype(jnp.float32)
    returned = lax.all_to_all(
        products.reshape(axis_size, capacity), "expert", split_axis=0, concat_axis=0, tiled=True
    )
    expert_rows = jnp.sum(
        jnp.where(
            (routes[:, :, None] == expert_iota)[..., None], returned[None, None, :, :], 0.0
        ),
        axis=2,
    )
    answer = jnp.sum(
        jnp.where(pair_rank[..., None] == jnp.arange(capacity), expert_rows, 0.0), axis=2
    )
    gate_grad = (answer - jnp.sum(gate_share * answer, axis=1, keepdims=True)) / prob_sum

    outputs = jnp.stack(adam_update(weight, moment_one[0], moment_two[0], grad_sum))
    outputs = with_layout_constraint(outputs, Layout(major_to_minor=(0, 1, 2)))
    outputs, gate_grad = lax.optimization_barrier((outputs, gate_grad))

    mine = partner[me]
    levels = axis_size.bit_length() - 1
    device_iota = jnp.arange(expert_count, dtype=jnp.int32)
    which = jnp.int32(0)
    for level in range(levels):
        which = which + jnp.where(mine == (me ^ (1 << level)), level + 1, 0).astype(jnp.int32)

    def exchange(arrays, level, pairs=None):
        flip = 1 << level
        pairs = range(axis_size) if pairs is None else pairs
        return lax.ppermute(arrays, "expert", perm=[(i, i ^ flip) for i in pairs])

    optional = list(range(max(levels - 2, 0), levels))
    fixed = list(range(levels - len(optional)))
    cases = [outputs] + [exchange(outputs, level) for level in fixed]
    if optional:
        units = [(level, list(range(axis_size))) for level in optional[:-1]]
        top = optional[-1]
        other = optional[0] if len(optional) > 1 else None
        for value in range(2 if other is not None else 1):
            members = [i for i in range(axis_size) if other is None or (i >> other & 1) == value]
            units.append((top, members))
        choice = jnp.int32(0)
        member_of = []
        for position, (level, members) in enumerate(units):
            member_iota = jnp.asarray(members, dtype=jnp.int32)
            used = jnp.any(partner[member_iota] == (member_iota ^ (1 << level)))
            choice = choice + jnp.where(used, 1 << position, 0).astype(jnp.int32)
            member_of.append(jnp.any(member_iota == me))

        def branch(mask):
            def run(arrays):
                picks = [arrays]
                index = jnp.int32(0)
                for position, (level, members) in enumerate(units):
                    if mask >> position & 1:
                        picks.append(exchange(arrays, level, members))
                        hit = (which == level + 1) & member_of[position]
                        index = index + jnp.where(hit, len(picks) - 1, 0).astype(jnp.int32)
                return lax.select_n(index, *picks) if len(picks) > 1 else arrays

            return run

        cases[0] = lax.switch(choice, [branch(mask) for mask in range(1 << len(units))], outputs)
    top_index = jnp.where(which <= len(fixed), which, 0)
    landed = lax.select_n(top_index, *cases)
    return (gate_grad, landed[0][None], landed[1][None], landed[2][None])


def solution(mesh):
    in_specs = (
        P(("dp", "expert"), None),
        P(("dp", "expert"), None),
        P(("dp", "expert"), None),
        P("expert", "dp", None, None),
        P("expert", "dp", None),
        P("expert", "dp", None),
        P("expert", "dp", None),
        P(),
    )
    out_specs = (
        P(("dp", "expert"), None),
        P("expert", "dp", None),
        P("expert", "dp", None),
        P("expert", "dp", None),
    )
    return jax.shard_map(
        on_device, mesh=mesh, in_specs=in_specs, out_specs=out_specs, check_vma=False
    )
```

```python
import jax
import jax.numpy as jnp
from jax import lax
from jax.sharding import PartitionSpec as P
from jax.experimental.layout import Layout, with_layout_constraint

beta_one = 0.9
beta_two = 0.95
learn_rate = 0.001
weight_decay = 0.1
adam_epsilon = 1e-08
step_count = 1000

gather_limit_bytes = 16 * 1024 * 1024


def adam_update(weight, moment_first, moment_second, grad_sum):
    first_new = beta_one * moment_first.astype(jnp.float32) + (1.0 - beta_one) * grad_sum
    second_new = (
        beta_two * moment_second.astype(jnp.float32) + (1.0 - beta_two) * grad_sum * grad_sum
    )
    corr_one = 1.0 - beta_one**step_count
    corr_two = 1.0 - beta_two**step_count
    weight_full = weight.astype(jnp.float32)
    direction = first_new / corr_one / (jnp.sqrt(second_new / corr_two) + adam_epsilon)
    updated = weight_full - learn_rate * (direction + weight_decay * weight_full)
    return (
        updated.astype(jnp.bfloat16),
        first_new.astype(jnp.bfloat16),
        second_new.astype(jnp.bfloat16),
    )


def block_ranks(hit):
    return jnp.cumsum(hit.astype(jnp.int32), axis=-1) - 1


def slot_onehot(hit, rank, capacity):
    slot_iota = jnp.arange(capacity, dtype=jnp.int32)
    return hit[..., None, :] & (rank[..., None, :] == slot_iota[:, None])


def on_device(
    grad_out, routes, router_probs, saved_hidden, down_weight, moment_one, moment_two, partner
):
    tok_rows, top_count = routes.shape
    width = grad_out.shape[1]
    axis_size = lax.axis_size("expert")
    me = lax.axis_index("expert")
    expert_count = partner.shape[0]
    capacity = 3 * tok_rows * top_count // (2 * expert_count)
    slot_count = capacity * axis_size

    weight = down_weight[0]
    weight_full = lax.all_gather(weight, "dp", axis=0, tiled=True)
    hidden = saved_hidden[0, 0]

    prob_sum = jnp.sum(router_probs, axis=1, keepdims=True)
    gate_share = router_probs / prob_sum
    gate_low = gate_share.astype(jnp.bfloat16)

    expert_iota = jnp.arange(expert_count, dtype=jnp.int32)
    local_hit = jnp.any(routes[:, :, None] == expert_iota[None, None, :], axis=1)
    local_rank = block_ranks(local_hit.T).T
    pair_rank = jnp.take_along_axis(local_rank, routes, axis=1)

    gather_bytes = axis_size * tok_rows * width * grad_out.dtype.itemsize
    if gather_bytes <= gather_limit_bytes:
        packed = jnp.concatenate([routes.astype(jnp.float32), router_probs], axis=1)
        packed_all = lax.all_gather(packed, "expert", axis=0, tiled=True)
        half = width // 2 if width % 256 == 0 else width
        grad_all = lax.all_gather(grad_out[:, :half], "expert", axis=0, tiled=True)
        if half < width:
            send_onehot = slot_onehot(local_hit.T, local_rank.T, capacity)
            send_rows = jnp.einsum(
                "ejt,td->ejd",
                send_onehot.astype(jnp.bfloat16),
                grad_out[:, half:],
                preferred_element_type=jnp.float32,
            ).astype(jnp.bfloat16)
            received = lax.all_to_all(
                send_rows, "expert", split_axis=0, concat_axis=0, tiled=True
            )
        routes_all = packed_all[:, :top_count].astype(jnp.int32)
        probs_all = packed_all[:, top_count:]
        gate_all = (probs_all / jnp.sum(probs_all, axis=1, keepdims=True)).astype(jnp.bfloat16)
        hit_k = routes_all == me
        hit = jnp.any(hit_k, axis=1).reshape(axis_size, tok_rows)
        gate_tok = jnp.sum(
            jnp.where(hit_k, gate_all.astype(jnp.float32), 0.0), axis=1
        ).reshape(axis_size, tok_rows)
        onehot = slot_onehot(hit, block_ranks(hit), capacity)
        dispatched = jnp.einsum(
            "sjt,std->sjd",
            onehot.astype(jnp.bfloat16),
            grad_all.reshape(axis_size, tok_rows, half),
            preferred_element_type=jnp.float32,
        ).astype(jnp.bfloat16)
        if half < width:
            dispatched = jnp.concatenate([dispatched, received], axis=2)
        slot_gate = jnp.sum(
            jnp.where(onehot, gate_tok[:, None, :], 0.0), axis=2
        ).astype(jnp.bfloat16)
    else:
        gate_pair = jnp.sum(
            jnp.where(
                routes[:, :, None] == expert_iota[None, None, :],
                gate_low.astype(jnp.float32)[:, :, None],
                0.0,
            ),
            axis=1,
        )
        onehot = slot_onehot(local_hit.T, local_rank.T, capacity)
        send_rows = jnp.einsum(
            "ejt,td->ejd",
            onehot.astype(jnp.bfloat16),
            grad_out,
            preferred_element_type=jnp.float32,
        ).astype(jnp.bfloat16)
        send_gate = jnp.sum(jnp.where(onehot, gate_pair.T[:, None, :], 0.0), axis=2).astype(
            jnp.bfloat16
        )
        dispatched = lax.all_to_all(send_rows, "expert", split_axis=0, concat_axis=0, tiled=True)
        slot_gate = lax.all_to_all(send_gate, "expert", split_axis=0, concat_axis=0, tiled=True)

    dispatched = dispatched.reshape(slot_count, width)
    slot_gate = slot_gate.reshape(slot_count)
    scaled = slot_gate[:, None] * dispatched
    projected = lax.dot_general(
        dispatched,
        weight_full,
        (((1,), (1,)), ((), ())),
        preferred_element_type=jnp.float32,
    )
    products = jnp.sum(hidden.astype(jnp.float32) * projected, axis=1)
    grad_full = lax.dot_general(
        hidden, scaled, (((0,), (0,)), ((), ())), preferred_element_type=jnp.float32
    ).astype(jnp.bfloat16)
    grad_full = with_layout_constraint(grad_full, Layout(major_to_minor=(0, 1)))
    grad_sum = lax.psum_scatter(
        grad_full,
        "dp",
        scatter_dimension=0,
        tiled=True,
    ).astype(jnp.float32)
    returned = lax.all_to_all(
        products.reshape(axis_size, capacity), "expert", split_axis=0, concat_axis=0, tiled=True
    )
    expert_rows = jnp.sum(
        jnp.where(
            (routes[:, :, None] == expert_iota)[..., None], returned[None, None, :, :], 0.0
        ),
        axis=2,
    )
    answer = jnp.sum(
        jnp.where(pair_rank[..., None] == jnp.arange(capacity), expert_rows, 0.0), axis=2
    )
    gate_grad = (answer - jnp.sum(gate_share * answer, axis=1, keepdims=True)) / prob_sum

    outputs = jnp.stack(adam_update(weight, moment_one[0], moment_two[0], grad_sum))
    outputs = with_layout_constraint(outputs, Layout(major_to_minor=(0, 1, 2)))
    outputs, gate_grad = lax.optimization_barrier((outputs, gate_grad))

    mine = partner[me]
    levels = axis_size.bit_length() - 1
    device_iota = jnp.arange(expert_count, dtype=jnp.int32)
    which = jnp.int32(0)
    for level in range(levels):
        which = which + jnp.where(mine == (me ^ (1 << level)), level + 1, 0).astype(jnp.int32)

    def exchange(arrays, level, pairs=None):
        flip = 1 << level
        pairs = range(axis_size) if pairs is None else pairs
        return lax.ppermute(arrays, "expert", perm=[(i, i ^ flip) for i in pairs])

    optional = list(range(max(levels - 2, 0), levels))
    fixed = list(range(levels - len(optional)))
    cases = [outputs] + [exchange(outputs, level) for level in fixed]
    if optional:
        units = [(level, list(range(axis_size))) for level in optional[:-1]]
        top = optional[-1]
        other = optional[0] if len(optional) > 1 else None
        for value in range(2 if other is not None else 1):
            members = [i for i in range(axis_size) if other is None or (i >> other & 1) == value]
            units.append((top, members))
        choice = jnp.int32(0)
        member_of = []
        for position, (level, members) in enumerate(units):
            member_iota = jnp.asarray(members, dtype=jnp.int32)
            used = jnp.any(partner[member_iota] == (member_iota ^ (1 << level)))
            choice = choice + jnp.where(used, 1 << position, 0).astype(jnp.int32)
            member_of.append(jnp.any(member_iota == me))

        def branch(mask):
            def run(arrays):
                picks = [arrays]
                index = jnp.int32(0)
                for position, (level, members) in enumerate(units):
                    if mask >> position & 1:
                        picks.append(exchange(arrays, level, members))
                        hit = (which == level + 1) & member_of[position]
                        index = index + jnp.where(hit, len(picks) - 1, 0).astype(jnp.int32)
                return lax.select_n(index, *picks) if len(picks) > 1 else arrays

            return run

        cases[0] = lax.switch(choice, [branch(mask) for mask in range(1 << len(units))], outputs)
    top_index = jnp.where(which <= len(fixed), which, 0)
    landed = lax.select_n(top_index, *cases)
    return (gate_grad, landed[0][None], landed[1][None], landed[2][None])


def solution(mesh):
    in_specs = (
        P(("dp", "expert"), None),
        P(("dp", "expert"), None),
        P(("dp", "expert"), None),
        P("expert", "dp", None, None),
        P("expert", "dp", None),
        P("expert", "dp", None),
        P("expert", "dp", None),
        P(),
    )
    out_specs = (
        P(("dp", "expert"), None),
        P("expert", "dp", None),
        P("expert", "dp", None),
        P("expert", "dp", None),
    )
    return jax.shard_map(
        on_device, mesh=mesh, in_specs=in_specs, out_specs=out_specs, check_vma=False
    )
```

```python
import jax
import jax.numpy as jnp
from jax import lax
from jax.sharding import PartitionSpec as P
from jax.experimental.layout import Layout, with_layout_constraint

beta_one = 0.9
beta_two = 0.95
learn_rate = 0.001
weight_decay = 0.1
adam_epsilon = 1e-08
step_count = 1000

gather_limit_bytes = 16 * 1024 * 1024


def adam_update(weight, moment_first, moment_second, grad_sum):
    first_new = beta_one * moment_first.astype(jnp.float32) + (1.0 - beta_one) * grad_sum
    second_new = (
        beta_two * moment_second.astype(jnp.float32) + (1.0 - beta_two) * grad_sum * grad_sum
    )
    corr_one = 1.0 - beta_one**step_count
    corr_two = 1.0 - beta_two**step_count
    weight_full = weight.astype(jnp.float32)
    direction = first_new / corr_one / (jnp.sqrt(second_new / corr_two) + adam_epsilon)
    updated = weight_full - learn_rate * (direction + weight_decay * weight_full)
    return (
        updated.astype(jnp.bfloat16),
        first_new.astype(jnp.bfloat16),
        second_new.astype(jnp.bfloat16),
    )


def block_ranks(hit):
    return jnp.cumsum(hit.astype(jnp.int32), axis=-1) - 1


def slot_onehot(hit, rank, capacity):
    slot_iota = jnp.arange(capacity, dtype=jnp.int32)
    return hit[..., None, :] & (rank[..., None, :] == slot_iota[:, None])


def on_device(
    grad_out, routes, router_probs, saved_hidden, down_weight, moment_one, moment_two, partner
):
    tok_rows, top_count = routes.shape
    width = grad_out.shape[1]
    axis_size = lax.axis_size("expert")
    me = lax.axis_index("expert")
    expert_count = partner.shape[0]
    capacity = 3 * tok_rows * top_count // (2 * expert_count)
    slot_count = capacity * axis_size

    weight = down_weight[0]
    weight_full = lax.all_gather(weight, "dp", axis=0, tiled=True)
    hidden = saved_hidden[0, 0]

    prob_sum = jnp.sum(router_probs, axis=1, keepdims=True)
    gate_share = router_probs / prob_sum
    gate_low = gate_share.astype(jnp.bfloat16)

    expert_iota = jnp.arange(expert_count, dtype=jnp.int32)
    local_hit = jnp.any(routes[:, :, None] == expert_iota[None, None, :], axis=1)
    local_rank = block_ranks(local_hit.T).T
    pair_rank = jnp.take_along_axis(local_rank, routes, axis=1)

    gather_bytes = axis_size * tok_rows * width * grad_out.dtype.itemsize
    if gather_bytes <= gather_limit_bytes:
        packed = jnp.concatenate([routes.astype(jnp.float32), router_probs], axis=1)
        packed_all = lax.all_gather(packed, "expert", axis=0, tiled=True)
        grad_all = lax.all_gather(grad_out, "expert", axis=0, tiled=True)
        routes_all = packed_all[:, :top_count].astype(jnp.int32)
        probs_all = packed_all[:, top_count:]
        gate_all = (probs_all / jnp.sum(probs_all, axis=1, keepdims=True)).astype(jnp.bfloat16)
        hit_k = routes_all == me
        hit = jnp.any(hit_k, axis=1).reshape(axis_size, tok_rows)
        gate_tok = jnp.sum(
            jnp.where(hit_k, gate_all.astype(jnp.float32), 0.0), axis=1
        ).reshape(axis_size, tok_rows)
        onehot = slot_onehot(hit, block_ranks(hit), capacity)
        dispatched = jnp.einsum(
            "sjt,std->sjd",
            onehot.astype(jnp.bfloat16),
            grad_all.reshape(axis_size, tok_rows, width),
            preferred_element_type=jnp.float32,
        ).astype(jnp.bfloat16)
        slot_gate = jnp.sum(
            jnp.where(onehot, gate_tok[:, None, :], 0.0), axis=2
        ).astype(jnp.bfloat16)
    else:
        gate_pair = jnp.sum(
            jnp.where(
                routes[:, :, None] == expert_iota[None, None, :],
                gate_low.astype(jnp.float32)[:, :, None],
                0.0,
            ),
            axis=1,
        )
        onehot = slot_onehot(local_hit.T, local_rank.T, capacity)
        send_rows = jnp.einsum(
            "ejt,td->ejd",
            onehot.astype(jnp.bfloat16),
            grad_out,
            preferred_element_type=jnp.float32,
        ).astype(jnp.bfloat16)
        send_gate = jnp.sum(jnp.where(onehot, gate_pair.T[:, None, :], 0.0), axis=2).astype(
            jnp.bfloat16
        )
        dispatched = lax.all_to_all(send_rows, "expert", split_axis=0, concat_axis=0, tiled=True)
        slot_gate = lax.all_to_all(send_gate, "expert", split_axis=0, concat_axis=0, tiled=True)

    dispatched = dispatched.reshape(slot_count, width)
    slot_gate = slot_gate.reshape(slot_count)
    scaled = slot_gate[:, None] * dispatched
    projected = lax.dot_general(
        dispatched,
        weight_full,
        (((1,), (1,)), ((), ())),
        preferred_element_type=jnp.float32,
    )
    products = jnp.sum(hidden.astype(jnp.float32) * projected, axis=1)
    grad_full = lax.dot_general(
        hidden, scaled, (((0,), (0,)), ((), ())), preferred_element_type=jnp.float32
    ).astype(jnp.bfloat16)
    grad_full = with_layout_constraint(grad_full, Layout(major_to_minor=(0, 1)))
    grad_sum = lax.psum_scatter(
        grad_full,
        "dp",
        scatter_dimension=0,
        tiled=True,
    ).astype(jnp.float32)
    returned = lax.all_to_all(
        products.reshape(axis_size, capacity), "expert", split_axis=0, concat_axis=0, tiled=True
    )
    expert_rows = jnp.sum(
        jnp.where(
            (routes[:, :, None] == expert_iota)[..., None], returned[None, None, :, :], 0.0
        ),
        axis=2,
    )
    answer = jnp.sum(
        jnp.where(pair_rank[..., None] == jnp.arange(capacity), expert_rows, 0.0), axis=2
    )
    gate_grad = (answer - jnp.sum(gate_share * answer, axis=1, keepdims=True)) / prob_sum

    outputs = jnp.stack(adam_update(weight, moment_one[0], moment_two[0], grad_sum))
    outputs = with_layout_constraint(outputs, Layout(major_to_minor=(0, 1, 2)))
    outputs, gate_grad = lax.optimization_barrier((outputs, gate_grad))

    mine = partner[me]
    levels = axis_size.bit_length() - 1
    device_iota = jnp.arange(expert_count, dtype=jnp.int32)
    which = jnp.int32(0)
    for level in range(levels):
        which = which + jnp.where(mine == (me ^ (1 << level)), level + 1, 0).astype(jnp.int32)

    def exchange(arrays, level, pairs=None):
        flip = 1 << level
        pairs = range(axis_size) if pairs is None else pairs
        return lax.ppermute(arrays, "expert", perm=[(i, i ^ flip) for i in pairs])

    optional = list(range(max(levels - 2, 0), levels))
    fixed = list(range(levels - len(optional)))
    cases = [outputs] + [exchange(outputs, level) for level in fixed]
    if optional:
        units = [(level, list(range(axis_size))) for level in optional[:-1]]
        top = optional[-1]
        other = optional[0] if len(optional) > 1 else None
        for value in range(2 if other is not None else 1):
            members = [i for i in range(axis_size) if other is None or (i >> other & 1) == value]
            units.append((top, members))
        choice = jnp.int32(0)
        member_of = []
        for position, (level, members) in enumerate(units):
            member_iota = jnp.asarray(members, dtype=jnp.int32)
            used = jnp.any(partner[member_iota] == (member_iota ^ (1 << level)))
            choice = choice + jnp.where(used, 1 << position, 0).astype(jnp.int32)
            member_of.append(jnp.any(member_iota == me))

        def branch(mask):
            def run(arrays):
                picks = [arrays]
                index = jnp.int32(0)
                for position, (level, members) in enumerate(units):
                    if mask >> position & 1:
                        picks.append(exchange(arrays, level, members))
                        hit = (which == level + 1) & member_of[position]
                        index = index + jnp.where(hit, len(picks) - 1, 0).astype(jnp.int32)
                return lax.select_n(index, *picks) if len(picks) > 1 else arrays

            return run

        cases[0] = lax.switch(choice, [branch(mask) for mask in range(1 << len(units))], outputs)
    top_index = jnp.where(which <= len(fixed), which, 0)
    landed = [lax.select_n(top_index, *[case[k][None] for case in cases]) for k in range(3)]
    return (gate_grad, landed[0], landed[1], landed[2])


def solution(mesh):
    in_specs = (
        P(("dp", "expert"), None),
        P(("dp", "expert"), None),
        P(("dp", "expert"), None),
        P("expert", "dp", None, None),
        P("expert", "dp", None),
        P("expert", "dp", None),
        P("expert", "dp", None),
        P(),
    )
    out_specs = (
        P(("dp", "expert"), None),
        P("expert", "dp", None),
        P("expert", "dp", None),
        P("expert", "dp", None),
    )
    return jax.shard_map(
        on_device, mesh=mesh, in_specs=in_specs, out_specs=out_specs, check_vma=False
    )
```

```python
import jax
import jax.numpy as jnp
from jax import lax
from jax.sharding import PartitionSpec as P
from jax.experimental.layout import Layout, with_layout_constraint

beta_one = 0.9
beta_two = 0.95
learn_rate = 0.001
weight_decay = 0.1
adam_epsilon = 1e-08
step_count = 1000

gather_limit_bytes = 16 * 1024 * 1024


def adam_update(weight, moment_first, moment_second, grad_sum):
    first_new = beta_one * moment_first.astype(jnp.float32) + (1.0 - beta_one) * grad_sum
    second_new = (
        beta_two * moment_second.astype(jnp.float32) + (1.0 - beta_two) * grad_sum * grad_sum
    )
    corr_one = 1.0 - beta_one**step_count
    corr_two = 1.0 - beta_two**step_count
    weight_full = weight.astype(jnp.float32)
    direction = first_new / corr_one / (jnp.sqrt(second_new / corr_two) + adam_epsilon)
    updated = weight_full - learn_rate * (direction + weight_decay * weight_full)
    return (
        updated.astype(jnp.bfloat16),
        first_new.astype(jnp.bfloat16),
        second_new.astype(jnp.bfloat16),
    )


def block_ranks(hit):
    return jnp.cumsum(hit.astype(jnp.int32), axis=-1) - 1


def slot_onehot(hit, rank, capacity):
    slot_iota = jnp.arange(capacity, dtype=jnp.int32)
    return hit[..., None, :] & (rank[..., None, :] == slot_iota[:, None])


def on_device(
    grad_out, routes, router_probs, saved_hidden, down_weight, moment_one, moment_two, partner
):
    tok_rows, top_count = routes.shape
    width = grad_out.shape[1]
    axis_size = lax.axis_size("expert")
    me = lax.axis_index("expert")
    expert_count = partner.shape[0]
    capacity = 3 * tok_rows * top_count // (2 * expert_count)
    slot_count = capacity * axis_size

    weight = down_weight[0]
    weight_full = lax.all_gather(weight, "dp", axis=0, tiled=True)
    hidden = saved_hidden[0, 0]

    prob_sum = jnp.sum(router_probs, axis=1, keepdims=True)
    gate_share = router_probs / prob_sum
    gate_low = gate_share.astype(jnp.bfloat16)

    expert_iota = jnp.arange(expert_count, dtype=jnp.int32)
    local_hit = jnp.any(routes[:, :, None] == expert_iota[None, None, :], axis=1)
    local_rank = block_ranks(local_hit.T).T
    pair_rank = jnp.take_along_axis(local_rank, routes, axis=1)

    gather_bytes = axis_size * tok_rows * width * grad_out.dtype.itemsize
    if gather_bytes <= gather_limit_bytes:
        packed = jnp.concatenate([routes.astype(jnp.float32), router_probs], axis=1)
        hidden_t, packed = lax.optimization_barrier((hidden.T, packed))
        packed_all = lax.all_gather(packed, "expert", axis=0, tiled=True)
        grad_all = lax.all_gather(grad_out, "expert", axis=0, tiled=True)
        routes_all = packed_all[:, :top_count].astype(jnp.int32)
        probs_all = packed_all[:, top_count:]
        gate_all = (probs_all / jnp.sum(probs_all, axis=1, keepdims=True)).astype(jnp.bfloat16)
        hit_k = routes_all == me
        hit = jnp.any(hit_k, axis=1).reshape(axis_size, tok_rows)
        gate_tok = jnp.sum(
            jnp.where(hit_k, gate_all.astype(jnp.float32), 0.0), axis=1
        ).reshape(axis_size, tok_rows)
        onehot = slot_onehot(hit, block_ranks(hit), capacity)
        dispatched = jnp.einsum(
            "sjt,std->sjd",
            onehot.astype(jnp.bfloat16),
            grad_all.reshape(axis_size, tok_rows, width),
            preferred_element_type=jnp.float32,
        ).astype(jnp.bfloat16)
        slot_gate = jnp.sum(
            jnp.where(onehot, gate_tok[:, None, :], 0.0), axis=2
        ).astype(jnp.bfloat16)
    else:
        hidden_t = hidden.T
        gate_pair = jnp.sum(
            jnp.where(
                routes[:, :, None] == expert_iota[None, None, :],
                gate_low.astype(jnp.float32)[:, :, None],
                0.0,
            ),
            axis=1,
        )
        onehot = slot_onehot(local_hit.T, local_rank.T, capacity)
        send_rows = jnp.einsum(
            "ejt,td->ejd",
            onehot.astype(jnp.bfloat16),
            grad_out,
            preferred_element_type=jnp.float32,
        ).astype(jnp.bfloat16)
        send_gate = jnp.sum(jnp.where(onehot, gate_pair.T[:, None, :], 0.0), axis=2).astype(
            jnp.bfloat16
        )
        dispatched = lax.all_to_all(send_rows, "expert", split_axis=0, concat_axis=0, tiled=True)
        slot_gate = lax.all_to_all(send_gate, "expert", split_axis=0, concat_axis=0, tiled=True)

    dispatched = dispatched.reshape(slot_count, width)
    slot_gate = slot_gate.reshape(slot_count)
    scaled = slot_gate[:, None] * dispatched
    projected = lax.dot_general(
        dispatched,
        weight_full,
        (((1,), (1,)), ((), ())),
        preferred_element_type=jnp.float32,
    )
    products = jnp.sum(hidden.astype(jnp.float32) * projected, axis=1)
    grad_full = lax.dot_general(
        hidden_t, scaled, (((1,), (0,)), ((), ())), preferred_element_type=jnp.float32
    ).astype(jnp.bfloat16)
    grad_full = with_layout_constraint(grad_full, Layout(major_to_minor=(0, 1)))
    grad_sum = lax.psum_scatter(
        grad_full,
        "dp",
        scatter_dimension=0,
        tiled=True,
    ).astype(jnp.float32)
    returned = lax.all_to_all(
        products.reshape(axis_size, capacity), "expert", split_axis=0, concat_axis=0, tiled=True
    )
    expert_rows = jnp.sum(
        jnp.where(
            (routes[:, :, None] == expert_iota)[..., None], returned[None, None, :, :], 0.0
        ),
        axis=2,
    )
    answer = jnp.sum(
        jnp.where(pair_rank[..., None] == jnp.arange(capacity), expert_rows, 0.0), axis=2
    )
    gate_grad = (answer - jnp.sum(gate_share * answer, axis=1, keepdims=True)) / prob_sum

    outputs = jnp.stack(adam_update(weight, moment_one[0], moment_two[0], grad_sum))
    outputs = with_layout_constraint(outputs, Layout(major_to_minor=(0, 1, 2)))
    outputs, gate_grad = lax.optimization_barrier((outputs, gate_grad))

    mine = partner[me]
    levels = axis_size.bit_length() - 1
    device_iota = jnp.arange(expert_count, dtype=jnp.int32)
    which = jnp.int32(0)
    for level in range(levels):
        which = which + jnp.where(mine == (me ^ (1 << level)), level + 1, 0).astype(jnp.int32)

    def exchange(arrays, level, pairs=None):
        flip = 1 << level
        pairs = range(axis_size) if pairs is None else pairs
        return lax.ppermute(arrays, "expert", perm=[(i, i ^ flip) for i in pairs])

    optional = list(range(max(levels - 2, 0), levels))
    fixed = list(range(levels - len(optional)))
    cases = [outputs] + [exchange(outputs, level) for level in fixed]
    if optional:
        units = [(level, list(range(axis_size))) for level in optional[:-1]]
        top = optional[-1]
        other = optional[0] if len(optional) > 1 else None
        for value in range(2 if other is not None else 1):
            members = [i for i in range(axis_size) if other is None or (i >> other & 1) == value]
            units.append((top, members))
        choice = jnp.int32(0)
        member_of = []
        for position, (level, members) in enumerate(units):
            member_iota = jnp.asarray(members, dtype=jnp.int32)
            used = jnp.any(partner[member_iota] == (member_iota ^ (1 << level)))
            choice = choice + jnp.where(used, 1 << position, 0).astype(jnp.int32)
            member_of.append(jnp.any(member_iota == me))

        def branch(mask):
            def run(arrays):
                picks = [arrays]
                index = jnp.int32(0)
                for position, (level, members) in enumerate(units):
                    if mask >> position & 1:
                        picks.append(exchange(arrays, level, members))
                        hit = (which == level + 1) & member_of[position]
                        index = index + jnp.where(hit, len(picks) - 1, 0).astype(jnp.int32)
                return lax.select_n(index, *picks) if len(picks) > 1 else arrays

            return run

        cases[0] = lax.switch(choice, [branch(mask) for mask in range(1 << len(units))], outputs)
    top_index = jnp.where(which <= len(fixed), which, 0)
    landed = lax.select_n(top_index, *cases)
    return (gate_grad, landed[0][None], landed[1][None], landed[2][None])


def solution(mesh):
    in_specs = (
        P(("dp", "expert"), None),
        P(("dp", "expert"), None),
        P(("dp", "expert"), None),
        P("expert", "dp", None, None),
        P("expert", "dp", None),
        P("expert", "dp", None),
        P("expert", "dp", None),
        P(),
    )
    out_specs = (
        P(("dp", "expert"), None),
        P("expert", "dp", None),
        P("expert", "dp", None),
        P("expert", "dp", None),
    )
    return jax.shard_map(
        on_device, mesh=mesh, in_specs=in_specs, out_specs=out_specs, check_vma=False
    )
```

```python
import jax
import jax.numpy as jnp
from jax import lax
from jax.sharding import PartitionSpec as P
from jax.experimental.layout import Layout, with_layout_constraint

beta_one = 0.9
beta_two = 0.95
learn_rate = 0.001
weight_decay = 0.1
adam_epsilon = 1e-08
step_count = 1000

gather_limit_bytes = 16 * 1024 * 1024


def adam_update(weight, moment_first, moment_second, grad_sum):
    first_new = beta_one * moment_first.astype(jnp.float32) + (1.0 - beta_one) * grad_sum
    second_new = (
        beta_two * moment_second.astype(jnp.float32) + (1.0 - beta_two) * grad_sum * grad_sum
    )
    corr_one = 1.0 - beta_one**step_count
    corr_two = 1.0 - beta_two**step_count
    weight_full = weight.astype(jnp.float32)
    direction = first_new / corr_one / (jnp.sqrt(second_new / corr_two) + adam_epsilon)
    updated = weight_full - learn_rate * (direction + weight_decay * weight_full)
    return (
        updated.astype(jnp.bfloat16),
        first_new.astype(jnp.bfloat16),
        second_new.astype(jnp.bfloat16),
    )


def block_ranks(hit):
    return jnp.cumsum(hit.astype(jnp.int32), axis=-1) - 1


def slot_onehot(hit, rank, capacity):
    slot_iota = jnp.arange(capacity, dtype=jnp.int32)
    return hit[..., None, :] & (rank[..., None, :] == slot_iota[:, None])


def on_device(
    grad_out, routes, router_probs, saved_hidden, down_weight, moment_one, moment_two, partner
):
    tok_rows, top_count = routes.shape
    width = grad_out.shape[1]
    axis_size = lax.axis_size("expert")
    me = lax.axis_index("expert")
    expert_count = partner.shape[0]
    capacity = 3 * tok_rows * top_count // (2 * expert_count)
    slot_count = capacity * axis_size

    weight = down_weight[0]
    weight_full = lax.all_gather(weight, "dp", axis=0, tiled=True)
    hidden = saved_hidden[0, 0]

    prob_sum = jnp.sum(router_probs, axis=1, keepdims=True)
    gate_share = router_probs / prob_sum
    gate_low = gate_share.astype(jnp.bfloat16)

    expert_iota = jnp.arange(expert_count, dtype=jnp.int32)
    local_hit = jnp.any(routes[:, :, None] == expert_iota[None, None, :], axis=1)
    local_rank = block_ranks(local_hit.T).T
    pair_rank = jnp.take_along_axis(local_rank, routes, axis=1)

    mine = partner[me]
    levels = axis_size.bit_length() - 1
    device_iota = jnp.arange(expert_count, dtype=jnp.int32)
    which = jnp.int32(0)
    for level in range(levels):
        which = which + jnp.where(mine == (me ^ (1 << level)), level + 1, 0).astype(jnp.int32)

    optional = list(range(max(levels - 2, 0), levels))
    fixed = list(range(levels - len(optional)))
    units = []
    choice = jnp.int32(0)
    member_of = []
    if optional:
        units += [(level, list(range(axis_size))) for level in optional[:-1]]
        top = optional[-1]
        other = optional[0] if len(optional) > 1 else None
        for value in range(2 if other is not None else 1):
            members = [i for i in range(axis_size) if other is None or (i >> other & 1) == value]
            units.append((top, members))
        for position, (level, members) in enumerate(units):
            member_iota = jnp.asarray(members, dtype=jnp.int32)
            used = jnp.any(partner[member_iota] == (member_iota ^ (1 << level)))
            choice = choice + jnp.where(used, 1 << position, 0).astype(jnp.int32)
            member_of.append(jnp.any(member_iota == me))


    gather_bytes = axis_size * tok_rows * width * grad_out.dtype.itemsize
    if gather_bytes <= gather_limit_bytes:
        packed = jnp.concatenate([routes.astype(jnp.float32), router_probs], axis=1)
        hidden_t, packed = lax.optimization_barrier((hidden.T, packed))
        packed_all = lax.all_gather(packed, "expert", axis=0, tiled=True)
        grad_all = lax.all_gather(grad_out, "expert", axis=0, tiled=True)
        routes_all = packed_all[:, :top_count].astype(jnp.int32)
        probs_all = packed_all[:, top_count:]
        gate_all = (probs_all / jnp.sum(probs_all, axis=1, keepdims=True)).astype(jnp.bfloat16)
        hit_k = routes_all == me
        hit = jnp.any(hit_k, axis=1).reshape(axis_size, tok_rows)
        gate_tok = jnp.sum(
            jnp.where(hit_k, gate_all.astype(jnp.float32), 0.0), axis=1
        ).reshape(axis_size, tok_rows)
        onehot = slot_onehot(hit, block_ranks(hit), capacity)
        dispatched = jnp.einsum(
            "sjt,std->sjd",
            onehot.astype(jnp.bfloat16),
            grad_all.reshape(axis_size, tok_rows, width),
            preferred_element_type=jnp.float32,
        ).astype(jnp.bfloat16)
        slot_gate = jnp.sum(
            jnp.where(onehot, gate_tok[:, None, :], 0.0), axis=2
        ).astype(jnp.bfloat16)
    else:
        hidden_t = hidden.T
        gate_pair = jnp.sum(
            jnp.where(
                routes[:, :, None] == expert_iota[None, None, :],
                gate_low.astype(jnp.float32)[:, :, None],
                0.0,
            ),
            axis=1,
        )
        onehot = slot_onehot(local_hit.T, local_rank.T, capacity)
        send_rows = jnp.einsum(
            "ejt,td->ejd",
            onehot.astype(jnp.bfloat16),
            grad_out,
            preferred_element_type=jnp.float32,
        ).astype(jnp.bfloat16)
        send_gate = jnp.sum(jnp.where(onehot, gate_pair.T[:, None, :], 0.0), axis=2).astype(
            jnp.bfloat16
        )
        dispatched = lax.all_to_all(send_rows, "expert", split_axis=0, concat_axis=0, tiled=True)
        slot_gate = lax.all_to_all(send_gate, "expert", split_axis=0, concat_axis=0, tiled=True)

    dispatched = dispatched.reshape(slot_count, width)
    dispatched, which, choice, member_of = lax.optimization_barrier(
        (dispatched, which, choice, member_of)
    )
    slot_gate = slot_gate.reshape(slot_count)
    scaled = slot_gate[:, None] * dispatched
    projected = lax.dot_general(
        dispatched,
        weight_full,
        (((1,), (1,)), ((), ())),
        preferred_element_type=jnp.float32,
    )
    products = jnp.sum(hidden.astype(jnp.float32) * projected, axis=1)
    grad_full = lax.dot_general(
        hidden_t, scaled, (((1,), (0,)), ((), ())), preferred_element_type=jnp.float32
    ).astype(jnp.bfloat16)
    grad_full = with_layout_constraint(grad_full, Layout(major_to_minor=(0, 1)))
    grad_sum = lax.psum_scatter(
        grad_full,
        "dp",
        scatter_dimension=0,
        tiled=True,
    ).astype(jnp.float32)
    returned = lax.all_to_all(
        products.reshape(axis_size, capacity), "expert", split_axis=0, concat_axis=0, tiled=True
    )
    expert_rows = jnp.sum(
        jnp.where(
            (routes[:, :, None] == expert_iota)[..., None], returned[None, None, :, :], 0.0
        ),
        axis=2,
    )
    answer = jnp.sum(
        jnp.where(pair_rank[..., None] == jnp.arange(capacity), expert_rows, 0.0), axis=2
    )
    gate_grad = (answer - jnp.sum(gate_share * answer, axis=1, keepdims=True)) / prob_sum

    outputs = jnp.stack(adam_update(weight, moment_one[0], moment_two[0], grad_sum))
    outputs = with_layout_constraint(outputs, Layout(major_to_minor=(0, 1, 2)))
    outputs, gate_grad = lax.optimization_barrier((outputs, gate_grad))

    def exchange(arrays, level, pairs=None):
        flip = 1 << level
        pairs = range(axis_size) if pairs is None else pairs
        return lax.ppermute(arrays, "expert", perm=[(i, i ^ flip) for i in pairs])

    cases = [outputs] + [exchange(outputs, level) for level in fixed]
    if optional:
        def branch(mask):
            def run(arrays):
                picks = [arrays]
                index = jnp.int32(0)
                for position, (level, members) in enumerate(units):
                    if mask >> position & 1:
                        picks.append(exchange(arrays, level, members))
                        hit = (which == level + 1) & member_of[position]
                        index = index + jnp.where(hit, len(picks) - 1, 0).astype(jnp.int32)
                return lax.select_n(index, *picks) if len(picks) > 1 else arrays

            return run

        cases[0] = lax.switch(choice, [branch(mask) for mask in range(1 << len(units))], outputs)
    top_index = jnp.where(which <= len(fixed), which, 0)
    landed = lax.select_n(top_index, *cases)
    return (gate_grad, landed[0][None], landed[1][None], landed[2][None])


def solution(mesh):
    in_specs = (
        P(("dp", "expert"), None),
        P(("dp", "expert"), None),
        P(("dp", "expert"), None),
        P("expert", "dp", None, None),
        P("expert", "dp", None),
        P("expert", "dp", None),
        P("expert", "dp", None),
        P(),
    )
    out_specs = (
        P(("dp", "expert"), None),
        P("expert", "dp", None),
        P("expert", "dp", None),
        P("expert", "dp", None),
    )
    return jax.shard_map(
        on_device, mesh=mesh, in_specs=in_specs, out_specs=out_specs, check_vma=False
    )
```

```python
import jax
import jax.numpy as jnp
from jax import lax
from jax.sharding import PartitionSpec as P
from jax.experimental.layout import Layout, with_layout_constraint

beta_one = 0.9
beta_two = 0.95
learn_rate = 0.001
weight_decay = 0.1
adam_epsilon = 1e-08
step_count = 1000

gather_limit_bytes = 16 * 1024 * 1024


def adam_update(weight, moment_first, moment_second, grad_sum):
    first_new = beta_one * moment_first.astype(jnp.float32) + (1.0 - beta_one) * grad_sum
    second_new = (
        beta_two * moment_second.astype(jnp.float32) + (1.0 - beta_two) * grad_sum * grad_sum
    )
    corr_one = 1.0 - beta_one**step_count
    corr_two = 1.0 - beta_two**step_count
    weight_full = weight.astype(jnp.float32)
    direction = first_new / corr_one / (jnp.sqrt(second_new / corr_two) + adam_epsilon)
    updated = weight_full - learn_rate * (direction + weight_decay * weight_full)
    return (
        updated.astype(jnp.bfloat16),
        first_new.astype(jnp.bfloat16),
        second_new.astype(jnp.bfloat16),
    )


def block_ranks(hit):
    return jnp.cumsum(hit.astype(jnp.int32), axis=-1) - 1


def slot_onehot(hit, rank, capacity):
    slot_iota = jnp.arange(capacity, dtype=jnp.int32)
    return hit[..., None, :] & (rank[..., None, :] == slot_iota[:, None])


def on_device(
    grad_out, routes, router_probs, saved_hidden, down_weight, moment_one, moment_two, partner
):
    tok_rows, top_count = routes.shape
    width = grad_out.shape[1]
    axis_size = lax.axis_size("expert")
    me = lax.axis_index("expert")
    expert_count = partner.shape[0]
    capacity = 3 * tok_rows * top_count // (2 * expert_count)
    slot_count = capacity * axis_size

    weight = down_weight[0]
    weight_full = lax.all_gather(weight, "dp", axis=0, tiled=True)
    hidden = saved_hidden[0, 0]

    prob_sum = jnp.sum(router_probs, axis=1, keepdims=True)
    gate_share = router_probs / prob_sum
    gate_low = gate_share.astype(jnp.bfloat16)

    expert_iota = jnp.arange(expert_count, dtype=jnp.int32)
    local_hit = jnp.any(routes[:, :, None] == expert_iota[None, None, :], axis=1)
    local_rank = block_ranks(local_hit.T).T
    pair_rank = jnp.take_along_axis(local_rank, routes, axis=1)

    mine = partner[me]
    levels = axis_size.bit_length() - 1
    device_iota = jnp.arange(expert_count, dtype=jnp.int32)
    which = jnp.int32(0)
    for level in range(levels):
        which = which + jnp.where(mine == (me ^ (1 << level)), level + 1, 0).astype(jnp.int32)

    optional = list(range(max(levels - 2, 0), levels))
    fixed = list(range(levels - len(optional)))
    units = []
    choice = jnp.int32(0)
    member_of = []
    if optional:
        units += [(level, list(range(axis_size))) for level in optional[:-1]]
        top = optional[-1]
        other = optional[0] if len(optional) > 1 else None
        for value in range(2 if other is not None else 1):
            members = [i for i in range(axis_size) if other is None or (i >> other & 1) == value]
            units.append((top, members))
        for position, (level, members) in enumerate(units):
            member_iota = jnp.asarray(members, dtype=jnp.int32)
            used = jnp.any(partner[member_iota] == (member_iota ^ (1 << level)))
            choice = choice + jnp.where(used, 1 << position, 0).astype(jnp.int32)
            member_of.append(jnp.any(member_iota == me))


    gather_bytes = axis_size * tok_rows * width * grad_out.dtype.itemsize
    if gather_bytes <= gather_limit_bytes:
        packed = jnp.concatenate([routes.astype(jnp.float32), router_probs], axis=1)
        hidden_t, packed = lax.optimization_barrier((hidden.T, packed))
        packed_all = lax.all_gather(packed, "expert", axis=0, tiled=True)
        grad_all = lax.all_gather(grad_out, "expert", axis=0, tiled=True)
        routes_all = packed_all[:, :top_count].astype(jnp.int32)
        probs_all = packed_all[:, top_count:]
        gate_all = (probs_all / jnp.sum(probs_all, axis=1, keepdims=True)).astype(jnp.bfloat16)
        hit_k = routes_all == me
        hit = jnp.any(hit_k, axis=1).reshape(axis_size, tok_rows)
        gate_tok = jnp.sum(
            jnp.where(hit_k, gate_all.astype(jnp.float32), 0.0), axis=1
        ).reshape(axis_size, tok_rows)
        onehot = slot_onehot(hit, block_ranks(hit), capacity)
        dispatched = jnp.einsum(
            "sjt,std->sjd",
            onehot.astype(jnp.bfloat16),
            grad_all.reshape(axis_size, tok_rows, width),
            preferred_element_type=jnp.float32,
        ).astype(jnp.bfloat16)
        slot_gate = jnp.sum(
            jnp.where(onehot, gate_tok[:, None, :], 0.0), axis=2
        ).astype(jnp.bfloat16)
    else:
        hidden_t = hidden.T
        gate_pair = jnp.sum(
            jnp.where(
                routes[:, :, None] == expert_iota[None, None, :],
                gate_low.astype(jnp.float32)[:, :, None],
                0.0,
            ),
            axis=1,
        )
        onehot = slot_onehot(local_hit.T, local_rank.T, capacity)
        send_rows = jnp.einsum(
            "ejt,td->ejd",
            onehot.astype(jnp.bfloat16),
            grad_out,
            preferred_element_type=jnp.float32,
        ).astype(jnp.bfloat16)
        send_gate = jnp.sum(jnp.where(onehot, gate_pair.T[:, None, :], 0.0), axis=2).astype(
            jnp.bfloat16
        )
        dispatched = lax.all_to_all(send_rows, "expert", split_axis=0, concat_axis=0, tiled=True)
        slot_gate = lax.all_to_all(send_gate, "expert", split_axis=0, concat_axis=0, tiled=True)

    dispatched = dispatched.reshape(slot_count, width)
    dispatched, which, choice, member_of = lax.optimization_barrier(
        (dispatched, which, choice, member_of)
    )
    slot_gate = slot_gate.reshape(slot_count)
    scaled = slot_gate[:, None] * dispatched
    projected = lax.dot_general(
        dispatched,
        weight_full,
        (((1,), (1,)), ((), ())),
        preferred_element_type=jnp.float32,
    )
    products = jnp.sum(hidden.astype(jnp.float32) * projected, axis=1)
    grad_full = lax.dot_general(
        hidden_t, scaled, (((1,), (0,)), ((), ())), preferred_element_type=jnp.float32
    ).astype(jnp.bfloat16)
    grad_full = with_layout_constraint(grad_full, Layout(major_to_minor=(0, 1)))
    grad_sum = lax.psum_scatter(
        grad_full,
        "dp",
        scatter_dimension=0,
        tiled=True,
    ).astype(jnp.float32)
    outputs = jnp.stack(adam_update(weight, moment_one[0], moment_two[0], grad_sum))
    outputs = with_layout_constraint(outputs, Layout(major_to_minor=(0, 1, 2)))
    returned = lax.all_to_all(
        products.reshape(axis_size, capacity), "expert", split_axis=0, concat_axis=0, tiled=True
    )
    outputs, returned = lax.optimization_barrier((outputs, returned))
    expert_rows = jnp.sum(
        jnp.where(
            (routes[:, :, None] == expert_iota)[..., None], returned[None, None, :, :], 0.0
        ),
        axis=2,
    )
    answer = jnp.sum(
        jnp.where(pair_rank[..., None] == jnp.arange(capacity), expert_rows, 0.0), axis=2
    )
    gate_grad = (answer - jnp.sum(gate_share * answer, axis=1, keepdims=True)) / prob_sum


    def exchange(arrays, level, pairs=None):
        flip = 1 << level
        pairs = range(axis_size) if pairs is None else pairs
        return lax.ppermute(arrays, "expert", perm=[(i, i ^ flip) for i in pairs])

    cases = [outputs] + [exchange(outputs, level) for level in fixed]
    if optional:
        def branch(mask):
            def run(arrays):
                picks = [arrays]
                index = jnp.int32(0)
                for position, (level, members) in enumerate(units):
                    if mask >> position & 1:
                        picks.append(exchange(arrays, level, members))
                        hit = (which == level + 1) & member_of[position]
                        index = index + jnp.where(hit, len(picks) - 1, 0).astype(jnp.int32)
                return lax.select_n(index, *picks) if len(picks) > 1 else arrays

            return run

        cases[0] = lax.switch(choice, [branch(mask) for mask in range(1 << len(units))], outputs)
    top_index = jnp.where(which <= len(fixed), which, 0)
    landed = lax.select_n(top_index, *cases)
    return (gate_grad, landed[0][None], landed[1][None], landed[2][None])


def solution(mesh):
    in_specs = (
        P(("dp", "expert"), None),
        P(("dp", "expert"), None),
        P(("dp", "expert"), None),
        P("expert", "dp", None, None),
        P("expert", "dp", None),
        P("expert", "dp", None),
        P("expert", "dp", None),
        P(),
    )
    out_specs = (
        P(("dp", "expert"), None),
        P("expert", "dp", None),
        P("expert", "dp", None),
        P("expert", "dp", None),
    )
    return jax.shard_map(
        on_device, mesh=mesh, in_specs=in_specs, out_specs=out_specs, check_vma=False
    )
```
